256 devices in a mesh: tm: 4 (over y), space: 64 (over z, x, core).
Axes of the slice: x: 4, y: 4, z: 8, core: 2. Of those that a mesh axis runs over, the one named last changes fastest.
Arguments:
- fine_nodes: float32 [4, 3, 128, 128, 256], P('tm', None, 'space'), may hold values from -1.25 to 1.25
- fine_implicit: float32 [4, 3, 128, 128, 256], P('tm', None, 'space'), may hold values from -18 to 18
Outputs:
- new_nodes: float32 [4, 3, 128, 128, 256], P('tm', None, 'space')
- new_implicit: float32 [4, 2, 128, 128, 256], P('tm', None, 'space')
The draws below stay inside these ranges and needn't reach their ends.
All inputs are finite; a program needn't handle non-finite values.
Results may differ from the reference program's by a relative error of at most 0.00014.
Values sent between devices are 32-bit elements; how exact they have to be, the bound alone decides.
No kernel may reach another device: no remote copies, remote signals or barrier semaphores. Data moves between devices by JAX's collectives and lax.ppermute only.
A program may use at most 128 MiB of HBM per device.

```python
import math
import jax
import jax.numpy as jnp

NX = 128
NY = 128
NZ = 256
NODES = 3
SLICES = 4


def draw_fine_nodes(key, part):
    key_sign = jax.random.fold_in(key, 11)
    key_field = jax.random.fold_in(key, 12)
    bits = jax.random.randint(key_sign, (SLICES, 1, NX // 2, 1, 1, 1), 0, 2)
    signs = (2 * bits - 1).astype(jnp.float32)
    signs = jnp.broadcast_to(signs, (SLICES, NODES, NX // 2, 2, NY, NZ)).reshape(SLICES, NODES, NX, NY, NZ)
    field = jax.random.uniform(key_field, (SLICES, NODES, NX, NY, NZ), jnp.float32, -1.0, 1.0)
    return 1.1 * signs + 0.1 * field


def steps_of(stream_key, shape, pieces, low, high):
    level = 1.0
    for dim, parts in pieces:
        steps = jax.random.uniform(jax.random.fold_in(jax.random.fold_in(stream_key, 6), dim), (parts,), jnp.float32, low / len(pieces), high / len(pieces))
        level = level * jnp.repeat(jnp.exp(steps), shape[dim] // parts).reshape((-1,) + (1,) * (len(shape) - 1 - dim))
    return level


def noise(key, dims, scale, bound, pieces=(), kind=jnp.bfloat16):
    entries = jax.random.normal(key, dims, jnp.float32) * scale
    if len(pieces) > 0:
        entries = steps_of(key, dims, pieces, -0.22, 0.18) * entries
    return jnp.clip(entries, min=-bound, max=bound).astype(kind)


def setup_inputs(seed: int = 0) -> dict:
    key_list = jax.random.split(jax.random.key(seed), 3)
    fine_nodes = draw_fine_nodes(jax.random.fold_in(key_list[2], 71), 0)
    fine_implicit = noise(key_list[1], (SLICES, NODES, NX, NY, NZ), 3.0, 18.0, ((0, 4), (2, 64)), jnp.float32)
    return {"fine_nodes": fine_nodes, "fine_implicit": fine_implicit}


WEIGHTS = ((5.0 / 24.0, 1.0 / 3.0, -1.0 / 24.0), (-1.0 / 24.0, 1.0 / 3.0, 5.0 / 24.0))
EPS2 = 2.0


def react(u):
    return u - u * u * u


def restrict(stacked):
    k, a, b, c = stacked.shape
    return stacked.reshape(k, a // 2, 2, b // 2, 2, c // 2, 2).mean(axis=(2, 4, 6))


def coarse_rate(stacked):
    lap = jnp.roll(stacked, -1, 1) + jnp.roll(stacked, 1, 1)
    lap = lap + jnp.roll(stacked, -1, 2) + jnp.roll(stacked, 1, 2)
    lap = lap + jnp.roll(stacked, -1, 3) + jnp.roll(stacked, 1, 3)
    return EPS2 * ((lap - 6.0 * stacked) * 0.25) + react(stacked)


def spread(values, following, axis):
    middle = 0.5 * (values + following)
    both = jnp.stack([values, middle], axis=axis + 1)
    shape = list(values.shape)
    shape[axis] = shape[axis] * 2
    return both.reshape(shape)


def refine(stacked):
    out = spread(stacked, jnp.roll(stacked, -1, 1), 1)
    out = spread(out, jnp.roll(out, -1, 2), 2)
    return spread(out, jnp.roll(out, -1, 3), 3)


def wave_square(size):
    kappa = (2.0 * math.pi) * jnp.fft.fftfreq(size).astype(jnp.float32)
    return kappa * kappa


def coarse_sweep(start, rates, sums):
    first = start + 0.25 * (coarse_rate(start[None])[0] - rates[0]) + sums[0]
    second = first + 0.25 * (coarse_rate(first[None])[0] - rates[1]) + sums[1]
    return first, second


def reference(fine_nodes, fine_implicit):
    lam = wave_square(NX)[:, None, None] + wave_square(NY)[None, :, None] + wave_square(NZ)[None, None, :]
    factor = 1.0 / (1.0 + 0.5 * lam)
    node_list = []
    term_list = []
    previous_end = None
    for slot in range(SLICES):
        nodes = fine_nodes[slot]
        implicit = fine_implicit[slot]
        explicit_old = react(nodes)
        rates_old = explicit_old + implicit
        values = [nodes[0]]
        terms = [implicit[0]]
        for m in range(2):
            w = WEIGHTS[m]
            quad = 0.5 * (w[0] * rates_old[0] + w[1] * rates_old[1] + w[2] * rates_old[2])
            rhs = values[m] + 0.25 * (react(values[m]) - explicit_old[m]) - 0.25 * implicit[m + 1] + quad
            solved = jnp.real(jnp.fft.ifftn(jnp.fft.fftn(rhs) * factor)).astype(rhs.dtype)
            values.append(solved)
            terms.append((solved - rhs) * 4.0)
        fresh = jnp.stack(values)
        rates_new = react(fresh) + jnp.stack(terms)
        sums = restrict(jnp.stack([0.5 * (w[0] * rates_new[0] + w[1] * rates_new[1] + w[2] * rates_new[2]) for w in WEIGHTS]))
        coarse = restrict(fresh)
        rates_c = coarse_rate(coarse[:2])
        start = coarse[0] if slot == 0 else previous_end
        first, second = coarse_sweep(start, rates_c, sums)
        previous_end_new = second
        delta = jnp.stack([first - coarse[1], second - coarse[2]])
        corr = refine(delta)
        fixed_one = values[1] + corr[0]
        fixed_two = values[2] + corr[1]
        if slot == 0:
            head = nodes[0]
        else:
            head = node_list[slot - 1][2]
        node_list.append(jnp.stack([head, fixed_one, fixed_two]))
        term_list.append(jnp.stack([terms[1], terms[2]]))
        previous_end = previous_end_new
    return jnp.stack(node_list), jnp.stack(term_list)
```

```python
import math

import jax
import jax.numpy as jnp
from jax import lax
from jax.sharding import PartitionSpec as P

WEIGHTS = ((5.0 / 24.0, 1.0 / 3.0, -1.0 / 24.0), (-1.0 / 24.0, 1.0 / 3.0, 5.0 / 24.0))
EPS2 = 2.0
HIGHEST = lax.Precision.HIGHEST


def react(u):
    return u - u * u * u


def real_basis(size):
    rows = lax.broadcasted_iota(jnp.int32, (size, size), 0)
    cells = lax.broadcasted_iota(jnp.int32, (size, size), 1)
    half = size // 2
    freq = jnp.where(rows <= half, rows, rows - half)
    phase = (freq * cells % size).astype(jnp.float32) * (2.0 * math.pi / size)
    scale = jnp.where((rows == 0) | (rows == half), 1.0 / math.sqrt(size), math.sqrt(2.0 / size))
    return jnp.where(rows <= half, jnp.cos(phase), jnp.sin(phase)) * scale


def wave_square(index, size):
    half = size // 2
    freq = jnp.where(index <= half, index, index - half).astype(jnp.float32)
    kappa = freq * (2.0 * math.pi / size)
    return kappa * kappa


def interp_matrix(size):
    fine_rows = lax.broadcasted_iota(jnp.int32, (2 * size, size), 0)
    coarse_cols = lax.broadcasted_iota(jnp.int32, (2 * size, size), 1)
    base = fine_rows // 2
    odd = fine_rows % 2
    take_base = jnp.where(coarse_cols == base, jnp.where(odd == 0, 1.0, 0.5), 0.0)
    take_next = jnp.where((odd == 1) & (coarse_cols == (base + 1) % size), 0.5, 0.0)
    return (take_base + take_next).astype(jnp.float32)


def spectral_solve(rhs, basis_x, basis_y, basis_z, factor):
    planes, size_y, size_z = rhs.shape
    flat = jnp.dot(rhs.reshape(planes * size_y, size_z), basis_z.T, precision=HIGHEST)
    field = flat.reshape(planes, size_y, size_z)
    field = jnp.einsum("ky,xyz->kxz", basis_y, field, precision=HIGHEST)
    field = lax.all_to_all(field, "space", split_axis=0, concat_axis=1, tiled=True)
    field = jnp.einsum("kx,yxz->kyz", basis_x, field, precision=HIGHEST) * factor
    field = jnp.einsum("kx,kyz->xyz", basis_x, field, precision=HIGHEST)
    field = lax.all_to_all(field, "space", split_axis=0, concat_axis=1, tiled=True)
    field = jnp.matmul(basis_y.T, field, precision=HIGHEST)
    flat = jnp.dot(field.reshape(planes * size_y, size_z), basis_z, precision=HIGHEST)
    return flat.reshape(planes, size_y, size_z)


def pair_average(size):
    rows = lax.broadcasted_iota(jnp.int32, (size, size // 2), 0)
    cols = lax.broadcasted_iota(jnp.int32, (size, size // 2), 1)
    return jnp.where(rows // 2 == cols, 0.5, 0.0).astype(jnp.float32)


def restrict(fields):
    count, planes, size_y, size_z = fields.shape
    pairs = fields.reshape(count, planes // 2, 2, size_y, size_z)
    summed = (pairs[:, :, 0] + pairs[:, :, 1]) * 0.5
    flat = jnp.dot(summed.reshape(-1, size_z), pair_average(size_z), precision=HIGHEST)
    field = flat.reshape(count, planes // 2, size_y, size_z // 2)
    return jnp.einsum("ya,kpyz->kpaz", pair_average(size_y), field, precision=HIGHEST)


def fetch(value, offset, back):
    count = lax.axis_size("space")
    if back == 0:
        pairs = [((target + offset) % count, target) for target in range(count)]
        return lax.ppermute(value, "space", pairs)
    slices = lax.axis_size("tm")
    pairs = [
        ((slot - back) * count + (target + offset) % count, slot * count + target)
        for slot in range(back, slices)
        for target in range(count)
    ]
    return lax.ppermute(value, ("tm", "space"), pairs)


def halo(groups, back=0):
    local = groups[0][0].shape[0]
    reach = []
    for block, low, high in groups:
        reach.append((-(-low // local), -(-high // local)))
    lowest = max(r[0] for r in reach)
    highest = max(r[1] for r in reach)
    pieces = [[] for _ in groups]
    for offset in range(-lowest, highest + 1):
        wanted = [i for i, r in enumerate(reach) if -r[0] <= offset <= r[1]]
        if offset == 0 and back == 0:
            for i in wanted:
                pieces[i].append(groups[i][0])
            continue
        sizes = [groups[i][0].shape[1] for i in wanted]
        joined = jnp.concatenate([groups[i][0] for i in wanted], axis=1)
        got = fetch(joined, offset, back)
        at = 0
        for i, size in zip(wanted, sizes):
            pieces[i].append(got[:, at:at + size])
            at += size
    result = []
    for i, (block, low, high) in enumerate(groups):
        full = jnp.concatenate(pieces[i], axis=0)
        begin = reach[i][0] * local - low
        result.append(full[begin:begin + local + low + high])
    return result


def coarse_rate(ext):
    mid = ext[1:-1]
    lap = ext[2:] + ext[:-2]
    lap = lap + jnp.roll(mid, -1, 1) + jnp.roll(mid, 1, 1)
    lap = lap + jnp.roll(mid, -1, 2) + jnp.roll(mid, 1, 2)
    return EPS2 * ((lap - 6.0 * mid) * 0.25) + react(mid)


def spread(values, following, axis):
    middle = 0.5 * (values + following)
    both = jnp.stack([values, middle], axis=axis + 1)
    shape = list(values.shape)
    shape[axis] = shape[axis] * 2
    return both.reshape(shape)


def refine(stacked):
    matrix_y = interp_matrix(stacked.shape[2])
    matrix_z = interp_matrix(stacked.shape[3])
    both = jnp.einsum("kayc,zc->kayz", stacked, matrix_z, precision=HIGHEST)
    both = jnp.einsum("Yy,kayz->kaYz", matrix_y, both, precision=HIGHEST)
    planes = stacked.shape[1] - 1
    return spread(both[:, :planes], both[:, 1:], 1)


def coarse_sweep(start, rates, sums):
    first = start[1:-1] + 0.25 * (coarse_rate(start) - rates[0]) + sums[0]
    second = first[1:-1] + 0.25 * (coarse_rate(first) - rates[1]) + sums[1]
    return (first[1:-1], second)


def on_device(fine_nodes, fine_implicit):
    nodes = fine_nodes[0]
    implicit = fine_implicit[0]
    planes, size_y, size_z = (nodes.shape[1], nodes.shape[2], nodes.shape[3])
    devices = lax.axis_size("space")
    size_x = planes * devices
    local_y = size_y // devices
    basis_x = real_basis(size_x)
    basis_y = real_basis(size_y)
    basis_z = real_basis(size_z)
    columns = lax.axis_index("space") * local_y + lax.iota(jnp.int32, local_y)
    lam = wave_square(lax.iota(jnp.int32, size_x), size_x)[:, None, None]
    lam = lam + wave_square(columns, size_y)[None, :, None]
    lam = lam + wave_square(lax.iota(jnp.int32, size_z), size_z)[None, None, :]
    factor = 1.0 / (1.0 + 0.5 * lam)
    explicit_old = react(nodes)
    rates_old = explicit_old + implicit
    values = [nodes[0]]
    terms = [implicit[0]]
    for m in range(2):
        w = WEIGHTS[m]
        quad = 0.5 * (w[0] * rates_old[0] + w[1] * rates_old[1] + w[2] * rates_old[2])
        rhs = (
            values[m] + 0.25 * (react(values[m]) - explicit_old[m]) - 0.25 * implicit[m + 1] + quad
        )
        solved = spectral_solve(rhs, basis_x, basis_y, basis_z, factor)
        values.append(solved)
        terms.append((solved - rhs) * 4.0)
    fresh = jnp.stack(values)
    rates_new = react(fresh) + jnp.stack(terms)
    sums = [0.5 * (w[0] * rates_new[0] + w[1] * rates_new[1] + w[2] * rates_new[2]) for w in WEIGHTS]
    coarse = restrict(jnp.stack([values[0], values[1], values[2], sums[0], sums[1]]))
    by_plane = jnp.moveaxis(coarse, 1, 0)
    slot = lax.axis_index("tm")
    slices = lax.axis_size("tm")
    start_c, rest = halo([(by_plane[:, 0:1], 2, 3), (by_plane[:, 1:5], 1, 2)])
    start_c = start_c[:, 0]
    rates_c = (coarse_rate(start_c), coarse_rate(rest[:, 0]))
    sums_c = (rest[:, 2], rest[1:-1, 3])
    coarse_one = rest[1:-1, 0]
    coarse_two = rest[1:-1, 1]
    local = planes // 2
    previous_two = fetch(values[2], 0, 1)
    previous_coarse_two = fetch(coarse_two, 0, 1)
    start = start_c
    for section in range(slices - 1):
        first, second = coarse_sweep(start, rates_c, sums_c)
        received = halo([(second[:local][:, None], 2, 3)], back=1)[0][:, 0]
        start = jnp.where(slot == 0, start_c, received)
    first, second = coarse_sweep(start, rates_c, sums_c)
    delta = jnp.stack([first - coarse_one, second - coarse_two, start[2:3 + local] - previous_coarse_two])
    corr = refine(delta)
    fixed_one = values[1] + corr[0]
    fixed_two = values[2] + corr[1]
    head = jnp.where(slot == 0, nodes[0], previous_two + corr[2])
    return (jnp.stack([head, fixed_one, fixed_two])[None], jnp.stack([terms[1], terms[2]])[None])


def solution(mesh):
    return jax.shard_map(
        on_device,
        mesh=mesh,
        in_specs=(P("tm", None, "space", None, None), P("tm", None, "space", None, None)),
        out_specs=(P("tm", None, "space", None, None), P("tm", None, "space", None, None)),
        check_vma=False,
    )
```

```python
import math

import jax
import jax.numpy as jnp
from jax import lax
from jax.sharding import PartitionSpec as P

WEIGHTS = ((5.0 / 24.0, 1.0 / 3.0, -1.0 / 24.0), (-1.0 / 24.0, 1.0 / 3.0, 5.0 / 24.0))
EPS2 = 2.0
HIGHEST = lax.Precision.HIGHEST


def react(u):
    return u - u * u * u


def real_basis(size):
    rows = lax.broadcasted_iota(jnp.int32, (size, size), 0)
    cells = lax.broadcasted_iota(jnp.int32, (size, size), 1)
    half = size // 2
    freq = jnp.where(rows <= half, rows, rows - half)
    phase = (freq * cells % size).astype(jnp.float32) * (2.0 * math.pi / size)
    scale = jnp.where((rows == 0) | (rows == half), 1.0 / math.sqrt(size), math.sqrt(2.0 / size))
    return jnp.where(rows <= half, jnp.cos(phase), jnp.sin(phase)) * scale


def wave_square(index, size):
    half = size // 2
    freq = jnp.where(index <= half, index, index - half).astype(jnp.float32)
    kappa = freq * (2.0 * math.pi / size)
    return kappa * kappa


def interp_matrix(size):
    fine_rows = lax.broadcasted_iota(jnp.int32, (2 * size, size), 0)
    coarse_cols = lax.broadcasted_iota(jnp.int32, (2 * size, size), 1)
    base = fine_rows // 2
    odd = fine_rows % 2
    take_base = jnp.where(coarse_cols == base, jnp.where(odd == 0, 1.0, 0.5), 0.0)
    take_next = jnp.where((odd == 1) & (coarse_cols == (base + 1) % size), 0.5, 0.0)
    return (take_base + take_next).astype(jnp.float32)


def spectral_solve(rhs, basis_x, basis_y, basis_z, factor):
    planes, size_y, size_z = rhs.shape
    flat = jnp.dot(rhs.reshape(planes * size_y, size_z), basis_z.T, precision=HIGHEST)
    field = flat.reshape(planes, size_y, size_z)
    field = jnp.einsum("ky,xyz->kxz", basis_y, field, precision=HIGHEST)
    field = lax.all_to_all(field, "space", split_axis=0, concat_axis=1, tiled=True)
    field = jnp.einsum("kx,yxz->kyz", basis_x, field, precision=HIGHEST) * factor
    field = jnp.einsum("kx,kyz->xyz", basis_x, field, precision=HIGHEST)
    field = lax.all_to_all(field, "space", split_axis=0, concat_axis=1, tiled=True)
    field = jnp.matmul(basis_y.T, field, precision=HIGHEST)
    flat = jnp.dot(field.reshape(planes * size_y, size_z), basis_z, precision=HIGHEST)
    return flat.reshape(planes, size_y, size_z)


def pair_average(size):
    rows = lax.broadcasted_iota(jnp.int32, (size, size // 2), 0)
    cols = lax.broadcasted_iota(jnp.int32, (size, size // 2), 1)
    return jnp.where(rows // 2 == cols, 0.5, 0.0).astype(jnp.float32)


def restrict(fields):
    count, planes, size_y, size_z = fields.shape
    pairs = fields.reshape(count, planes // 2, 2, size_y, size_z)
    summed = (pairs[:, :, 0] + pairs[:, :, 1]) * 0.5
    flat = jnp.dot(summed.reshape(-1, size_z), pair_average(size_z), precision=HIGHEST)
    field = flat.reshape(count, planes // 2, size_y, size_z // 2)
    return jnp.einsum("ya,kpyz->kpaz", pair_average(size_y), field, precision=HIGHEST)


def fetch(value, offset, back):
    count = lax.axis_size("space")
    if back == 0:
        pairs = [((target + offset) % count, target) for target in range(count)]
        return lax.ppermute(value, "space", pairs)
    slices = lax.axis_size("tm")
    pairs = [
        ((slot - back) * count + (target + offset) % count, slot * count + target)
        for slot in range(back, slices)
        for target in range(count)
    ]
    return lax.ppermute(value, ("tm", "space"), pairs)


def cover(low, high, have, local, allowed):
    plan = []
    at = low
    while at < high:
        best = None
        for offset in allowed:
            first = offset * local - have[0]
            last = offset * local + local + have[1]
            if first <= at < last and (best is None or last > best[2]):
                best = (offset, first, last)
        if best is None:
            offset = (at + have[0]) // local
            best = (offset, offset * local - have[0], offset * local + local + have[1])
        upto = min(best[2], high)
        plan.append((best[0], at - best[1], upto - best[1]))
        at = upto
    return plan


def gather_bands(items, back=0):
    local = items[0][0].shape[0] - items[0][1][0] - items[0][1][1]
    allowed = [0] if back == 0 else []
    plans = []
    for band, have, want in items:
        plan = cover(-want[0], local + want[1], have, local, allowed)
        for offset, _, _ in plan:
            if offset not in allowed:
                allowed.append(offset)
        plans.append(plan)
    by_offset = {}
    for i, plan in enumerate(plans):
        for j, (offset, first, last) in enumerate(plan):
            by_offset.setdefault(offset, []).append((i, j, first, last))
    got = {}
    for offset, entries in by_offset.items():
        parts = [items[i][0][first:last] for i, j, first, last in entries]
        if offset == 0 and back == 0:
            for (i, j, first, last), part in zip(entries, parts):
                got[(i, j)] = part
            continue
        moved = fetch(jnp.concatenate(parts, axis=0), offset, back)
        at = 0
        for i, j, first, last in entries:
            got[(i, j)] = moved[at:at + last - first]
            at += last - first
    return [
        jnp.concatenate([got[(i, j)] for j in range(len(plan))], axis=0)
        for i, plan in enumerate(plans)
    ]


def coarse_rate(ext):
    mid = ext[1:-1]
    lap = ext[2:] + ext[:-2]
    lap = lap + jnp.roll(mid, -1, 1) + jnp.roll(mid, 1, 1)
    lap = lap + jnp.roll(mid, -1, 2) + jnp.roll(mid, 1, 2)
    return EPS2 * ((lap - 6.0 * mid) * 0.25) + react(mid)


def spread(values, following, axis):
    middle = 0.5 * (values + following)
    both = jnp.stack([values, middle], axis=axis + 1)
    shape = list(values.shape)
    shape[axis] = shape[axis] * 2
    return both.reshape(shape)


def refine(stacked):
    matrix_y = interp_matrix(stacked.shape[2])
    matrix_z = interp_matrix(stacked.shape[3])
    both = jnp.einsum("kayc,zc->kayz", stacked, matrix_z, precision=HIGHEST)
    both = jnp.einsum("Yy,kayz->kaYz", matrix_y, both, precision=HIGHEST)
    planes = stacked.shape[1] - 1
    return spread(both[:, :planes], both[:, 1:], 1)


def coarse_sweep(start, rates, sums):
    first = start[1:-1] + 0.25 * (coarse_rate(start) - rates[0]) + sums[0]
    second = first[1:-1] + 0.25 * (coarse_rate(first) - rates[1]) + sums[1]
    return (first[1:-1], second)


def on_device(fine_nodes, fine_implicit):
    nodes = fine_nodes[0]
    implicit = fine_implicit[0]
    planes, size_y, size_z = (nodes.shape[1], nodes.shape[2], nodes.shape[3])
    devices = lax.axis_size("space")
    size_x = planes * devices
    local_y = size_y // devices
    basis_x = real_basis(size_x)
    basis_y = real_basis(size_y)
    basis_z = real_basis(size_z)
    columns = lax.axis_index("space") * local_y + lax.iota(jnp.int32, local_y)
    lam = wave_square(lax.iota(jnp.int32, size_x), size_x)[:, None, None]
    lam = lam + wave_square(columns, size_y)[None, :, None]
    lam = lam + wave_square(lax.iota(jnp.int32, size_z), size_z)[None, None, :]
    factor = 1.0 / (1.0 + 0.5 * lam)
    explicit_old = react(nodes)
    rates_old = explicit_old + implicit
    values = [nodes[0]]
    terms = [implicit[0]]
    for m in range(2):
        w = WEIGHTS[m]
        quad = 0.5 * (w[0] * rates_old[0] + w[1] * rates_old[1] + w[2] * rates_old[2])
        rhs = (
            values[m] + 0.25 * (react(values[m]) - explicit_old[m]) - 0.25 * implicit[m + 1] + quad
        )
        solved = spectral_solve(rhs, basis_x, basis_y, basis_z, factor)
        values.append(solved)
        terms.append((solved - rhs) * 4.0)
    fresh = jnp.stack(values)
    rates_new = react(fresh) + jnp.stack(terms)
    sums = [0.5 * (w[0] * rates_new[0] + w[1] * rates_new[1] + w[2] * rates_new[2]) for w in WEIGHTS]
    coarse = restrict(jnp.stack([values[0], values[1], values[2], sums[0], sums[1]]))
    slot = lax.axis_index("tm")
    slices = lax.axis_size("tm")
    local = planes // 2
    near = gather_bands(
        [(coarse[0], (0, 0), (1, 1)), (coarse[1], (0, 0), (1, 1)), (coarse[3], (0, 0), (1, 1)),
         (coarse[4], (0, 0), (1, 1)), (coarse[2], (0, 0), (0, 1))]
    )
    previous_two = fetch(values[2], 0, 1)
    previous_two, near = lax.optimization_barrier((previous_two, near))
    coarse_two = near[4]
    wide = gather_bands(
        [(near[0], (1, 1), (4, 3)), (near[1], (1, 1), (3, 2)), (near[2], (1, 1), (3, 2)),
         (near[3], (1, 1), (2, 1))]
    )
    previous_coarse_two = fetch(coarse_two, 0, 1)
    previous_coarse_two, wide = lax.optimization_barrier((previous_coarse_two, wide))
    start_c = wide[0]
    rates_c = (coarse_rate(start_c), coarse_rate(wide[1]))
    sums_c = (wide[2], wide[3])
    coarse_one = wide[1][3:4 + local]
    start = start_c
    for section in range(slices - 1):
        first, second = coarse_sweep(start, rates_c, sums_c)
        received = gather_bands([(second, (2, 1), (4, 3))], back=1)[0]
        start = jnp.where(slot == 0, start_c, received)
    first, second = coarse_sweep(start, rates_c, sums_c)
    delta = jnp.stack(
        [first[2:3 + local] - coarse_one, second[2:3 + local] - coarse_two,
         start[4:5 + local] - previous_coarse_two]
    )
    corr = refine(delta)
    fixed_one = values[1] + corr[0]
    fixed_two = values[2] + corr[1]
    head = jnp.where(slot == 0, nodes[0], previous_two + corr[2])
    return (jnp.stack([head, fixed_one, fixed_two])[None], jnp.stack([terms[1], terms[2]])[None])


def solution(mesh):
    return jax.shard_map(
        on_device,
        mesh=mesh,
        in_specs=(P("tm", None, "space", None, None), P("tm", None, "space", None, None)),
        out_specs=(P("tm", None, "space", None, None), P("tm", None, "space", None, None)),
        check_vma=False,
    )
```

```python
import math

import jax
import jax.numpy as jnp
from jax import lax
from jax.sharding import PartitionSpec as P

WEIGHTS = ((5.0 / 24.0, 1.0 / 3.0, -1.0 / 24.0), (-1.0 / 24.0, 1.0 / 3.0, 5.0 / 24.0))
EPS2 = 2.0
HIGHEST = lax.Precision.HIGHEST
SPACE = ("outer", "inner")


def exchange(field):
    outer = lax.axis_size("outer")
    inner = lax.axis_size("inner")
    size, cols, rest = field.shape
    chunk = size // (outer * inner)
    parts = field.reshape(outer, inner, chunk, cols, rest)
    parts = lax.all_to_all(parts, "inner", 1, 1)
    parts = lax.all_to_all(parts, "outer", 0, 0)
    return jnp.transpose(parts, (2, 0, 1, 3, 4)).reshape(chunk, outer * inner * cols, rest)


def react(u):
    return u - u * u * u


def real_basis(size):
    rows = lax.broadcasted_iota(jnp.int32, (size, size), 0)
    cells = lax.broadcasted_iota(jnp.int32, (size, size), 1)
    half = size // 2
    freq = jnp.where(rows <= half, rows, rows - half)
    phase = (freq * cells % size).astype(jnp.float32) * (2.0 * math.pi / size)
    scale = jnp.where((rows == 0) | (rows == half), 1.0 / math.sqrt(size), math.sqrt(2.0 / size))
    return jnp.where(rows <= half, jnp.cos(phase), jnp.sin(phase)) * scale


def wave_square(index, size):
    half = size // 2
    freq = jnp.where(index <= half, index, index - half).astype(jnp.float32)
    kappa = freq * (2.0 * math.pi / size)
    return kappa * kappa


def interp_matrix(size):
    fine_rows = lax.broadcasted_iota(jnp.int32, (2 * size, size), 0)
    coarse_cols = lax.broadcasted_iota(jnp.int32, (2 * size, size), 1)
    base = fine_rows // 2
    odd = fine_rows % 2
    take_base = jnp.where(coarse_cols == base, jnp.where(odd == 0, 1.0, 0.5), 0.0)
    take_next = jnp.where((odd == 1) & (coarse_cols == (base + 1) % size), 0.5, 0.0)
    return (take_base + take_next).astype(jnp.float32)


def spectral_solve(rhs, basis_x, basis_y, basis_z, factor):
    planes, size_y, size_z = rhs.shape
    flat = jnp.dot(rhs.reshape(planes * size_y, size_z), basis_z.T, precision=HIGHEST)
    field = flat.reshape(planes, size_y, size_z)
    field = jnp.einsum("ky,xyz->kxz", basis_y, field, precision=HIGHEST)
    field = exchange(field)
    field = jnp.einsum("kx,yxz->kyz", basis_x, field, precision=HIGHEST) * factor
    field = jnp.einsum("kx,kyz->xyz", basis_x, field, precision=HIGHEST)
    field = exchange(field)
    field = jnp.matmul(basis_y.T, field, precision=HIGHEST)
    flat = jnp.dot(field.reshape(planes * size_y, size_z), basis_z, precision=HIGHEST)
    return flat.reshape(planes, size_y, size_z)


def pair_average(size):
    rows = lax.broadcasted_iota(jnp.int32, (size, size // 2), 0)
    cols = lax.broadcasted_iota(jnp.int32, (size, size // 2), 1)
    return jnp.where(rows // 2 == cols, 0.5, 0.0).astype(jnp.float32)


def restrict(fields):
    count, planes, size_y, size_z = fields.shape
    pairs = fields.reshape(count, planes // 2, 2, size_y, size_z)
    summed = (pairs[:, :, 0] + pairs[:, :, 1]) * 0.5
    flat = jnp.dot(summed.reshape(-1, size_z), pair_average(size_z), precision=HIGHEST)
    field = flat.reshape(count, planes // 2, size_y, size_z // 2)
    return jnp.einsum("ya,kpyz->kpaz", pair_average(size_y), field, precision=HIGHEST)


def fetch(value, offset, back):
    count = lax.axis_size(SPACE)
    if back == 0:
        pairs = [((target + offset) % count, target) for target in range(count)]
        return lax.ppermute(value, SPACE, pairs)
    slices = lax.axis_size("tm")
    pairs = [
        ((slot - back) * count + (target + offset) % count, slot * count + target)
        for slot in range(back, slices)
        for target in range(count)
    ]
    return lax.ppermute(value, ("tm",) + SPACE, pairs)


def cover(low, high, have, local, allowed):
    plan = []
    at = low
    while at < high:
        best = None
        for offset in allowed:
            first = offset * local - have[0]
            last = offset * local + local + have[1]
            if first <= at < last and (best is None or last > best[2]):
                best = (offset, first, last)
        if best is None:
            offset = (at + have[0]) // local
            best = (offset, offset * local - have[0], offset * local + local + have[1])
        upto = min(best[2], high)
        plan.append((best[0], at - best[1], upto - best[1]))
        at = upto
    return plan


def gather_bands(items, back=0):
    local = items[0][0].shape[0] - items[0][1][0] - items[0][1][1]
    allowed = [0] if back == 0 else []
    plans = []
    for band, have, want in items:
        plan = cover(-want[0], local + want[1], have, local, allowed)
        for offset, _, _ in plan:
            if offset not in allowed:
                allowed.append(offset)
        plans.append(plan)
    by_offset = {}
    for i, plan in enumerate(plans):
        for j, (offset, first, last) in enumerate(plan):
            by_offset.setdefault(offset, []).append((i, j, first, last))
    got = {}
    for offset, entries in by_offset.items():
        parts = [items[i][0][first:last] for i, j, first, last in entries]
        if offset == 0 and back == 0:
            for (i, j, first, last), part in zip(entries, parts):
                got[(i, j)] = part
            continue
        moved = fetch(jnp.concatenate(parts, axis=0), offset, back)
        at = 0
        for i, j, first, last in entries:
            got[(i, j)] = moved[at:at + last - first]
            at += last - first
    return [
        jnp.concatenate([got[(i, j)] for j in range(len(plan))], axis=0)
        for i, plan in enumerate(plans)
    ]


def coarse_rate(ext):
    mid = ext[1:-1]
    lap = ext[2:] + ext[:-2]
    lap = lap + jnp.roll(mid, -1, 1) + jnp.roll(mid, 1, 1)
    lap = lap + jnp.roll(mid, -1, 2) + jnp.roll(mid, 1, 2)
    return EPS2 * ((lap - 6.0 * mid) * 0.25) + react(mid)


def spread(values, following, axis):
    middle = 0.5 * (values + following)
    both = jnp.stack([values, middle], axis=axis + 1)
    shape = list(values.shape)
    shape[axis] = shape[axis] * 2
    return both.reshape(shape)


def refine(stacked):
    matrix_y = interp_matrix(stacked.shape[2])
    matrix_z = interp_matrix(stacked.shape[3])
    both = jnp.einsum("kayc,zc->kayz", stacked, matrix_z, precision=HIGHEST)
    both = jnp.einsum("Yy,kayz->kaYz", matrix_y, both, precision=HIGHEST)
    planes = stacked.shape[1] - 1
    return spread(both[:, :planes], both[:, 1:], 1)


def coarse_sweep(start, rates, sums):
    first = start[1:-1] + 0.25 * (coarse_rate(start) - rates[0]) + sums[0]
    second = first[1:-1] + 0.25 * (coarse_rate(first) - rates[1]) + sums[1]
    return (first[1:-1], second)


def on_device(fine_nodes, fine_implicit):
    nodes = fine_nodes[0]
    implicit = fine_implicit[0]
    planes, size_y, size_z = (nodes.shape[1], nodes.shape[2], nodes.shape[3])
    devices = lax.axis_size(SPACE)
    size_x = planes * devices
    local_y = size_y // devices
    basis_x = real_basis(size_x)
    basis_y = real_basis(size_y)
    basis_z = real_basis(size_z)
    columns = lax.axis_index(SPACE) * local_y + lax.iota(jnp.int32, local_y)
    lam = wave_square(lax.iota(jnp.int32, size_x), size_x)[:, None, None]
    lam = lam + wave_square(columns, size_y)[None, :, None]
    lam = lam + wave_square(lax.iota(jnp.int32, size_z), size_z)[None, None, :]
    factor = 1.0 / (1.0 + 0.5 * lam)
    explicit_old = react(nodes)
    rates_old = explicit_old + implicit
    values = [nodes[0]]
    terms = [implicit[0]]
    for m in range(2):
        w = WEIGHTS[m]
        quad = 0.5 * (w[0] * rates_old[0] + w[1] * rates_old[1] + w[2] * rates_old[2])
        rhs = (
            values[m] + 0.25 * (react(values[m]) - explicit_old[m]) - 0.25 * implicit[m + 1] + quad
        )
        solved = spectral_solve(rhs, basis_x, basis_y, basis_z, factor)
        values.append(solved)
        terms.append((solved - rhs) * 4.0)
    fresh = jnp.stack(values)
    rates_new = react(fresh) + jnp.stack(terms)
    sums = [0.5 * (w[0] * rates_new[0] + w[1] * rates_new[1] + w[2] * rates_new[2]) for w in WEIGHTS]
    coarse = restrict(jnp.stack([values[0], values[1], values[2], sums[0], sums[1]]))
    slot = lax.axis_index("tm")
    slices = lax.axis_size("tm")
    local = planes // 2
    near = gather_bands(
        [(coarse[0], (0, 0), (1, 1)), (coarse[1], (0, 0), (1, 1)), (coarse[3], (0, 0), (1, 1)),
         (coarse[4], (0, 0), (1, 1)), (coarse[2], (0, 0), (0, 1))]
    )
    previous_two = fetch(values[2], 0, 1)
    previous_two, near = lax.optimization_barrier((previous_two, near))
    coarse_two = near[4]
    wide = gather_bands(
        [(near[0], (1, 1), (4, 3)), (near[1], (1, 1), (3, 2)), (near[2], (1, 1), (3, 2)),
         (near[3], (1, 1), (2, 1))]
    )
    previous_coarse_two = fetch(coarse_two, 0, 1)
    previous_coarse_two, wide = lax.optimization_barrier((previous_coarse_two, wide))
    start_c = wide[0]
    rates_c = (coarse_rate(start_c), coarse_rate(wide[1]))
    sums_c = (wide[2], wide[3])
    coarse_one = wide[1][3:4 + local]
    start = start_c
    for section in range(slices - 1):
        first, second = coarse_sweep(start, rates_c, sums_c)
        received = gather_bands([(second, (2, 1), (4, 3))], back=1)[0]
        start = jnp.where(slot == 0, start_c, received)
    first, second = coarse_sweep(start, rates_c, sums_c)
    delta = jnp.stack(
        [first[2:3 + local] - coarse_one, second[2:3 + local] - coarse_two,
         start[4:5 + local] - previous_coarse_two]
    )
    corr = refine(delta)
    fixed_one = values[1] + corr[0]
    fixed_two = values[2] + corr[1]
    head = jnp.where(slot == 0, nodes[0], previous_two + corr[2])
    return (jnp.stack([head, fixed_one, fixed_two])[None], jnp.stack([terms[1], terms[2]])[None])


def solution(mesh):
    slices, devices = mesh.devices.shape
    inner = math.gcd(devices, 8)
    fine = jax.sharding.Mesh(mesh.devices.reshape(slices, devices // inner, inner), ("tm",) + SPACE)
    spec = P("tm", None, SPACE, None, None)
    return jax.shard_map(
        on_device, mesh=fine, in_specs=(spec, spec), out_specs=(spec, spec), check_vma=False
    )
```

```python
import math

import jax
import jax.numpy as jnp
from jax import lax
from jax.sharding import PartitionSpec as P

WEIGHTS = ((5.0 / 24.0, 1.0 / 3.0, -1.0 / 24.0), (-1.0 / 24.0, 1.0 / 3.0, 5.0 / 24.0))
EPS2 = 2.0
HIGHEST = lax.Precision.HIGHEST


def react(u):
    return u - u * u * u


def real_basis(size):
    rows = lax.broadcasted_iota(jnp.int32, (size, size), 0)
    cells = lax.broadcasted_iota(jnp.int32, (size, size), 1)
    half = size // 2
    freq = jnp.where(rows <= half, rows, rows - half)
    phase = (freq * cells % size).astype(jnp.float32) * (2.0 * math.pi / size)
    scale = jnp.where((rows == 0) | (rows == half), 1.0 / math.sqrt(size), math.sqrt(2.0 / size))
    return jnp.where(rows <= half, jnp.cos(phase), jnp.sin(phase)) * scale


def wave_square(index, size):
    half = size // 2
    freq = jnp.where(index <= half, index, index - half).astype(jnp.float32)
    kappa = freq * (2.0 * math.pi / size)
    return kappa * kappa


def interp_matrix(size):
    fine_rows = lax.broadcasted_iota(jnp.int32, (2 * size, size), 0)
    coarse_cols = lax.broadcasted_iota(jnp.int32, (2 * size, size), 1)
    base = fine_rows // 2
    odd = fine_rows % 2
    take_base = jnp.where(coarse_cols == base, jnp.where(odd == 0, 1.0, 0.5), 0.0)
    take_next = jnp.where((odd == 1) & (coarse_cols == (base + 1) % size), 0.5, 0.0)
    return (take_base + take_next).astype(jnp.float32)


def spectral_solve(rhs, basis_x, basis_y, basis_z, factor):
    planes, size_y, size_z = rhs.shape
    flat = jnp.dot(rhs.reshape(planes * size_y, size_z), basis_z.T, precision=HIGHEST)
    field = flat.reshape(planes, size_y, size_z)
    field = jnp.einsum("ky,xyz->kxz", basis_y, field, precision=HIGHEST)
    field = lax.all_to_all(field, "space", split_axis=0, concat_axis=1, tiled=True)
    field = jnp.einsum("kx,yxz->kyz", basis_x, field, precision=HIGHEST) * factor
    field = jnp.einsum("kx,kyz->xyz", basis_x, field, precision=HIGHEST)
    field = lax.all_to_all(field, "space", split_axis=0, concat_axis=1, tiled=True)
    field = jnp.matmul(basis_y.T, field, precision=HIGHEST)
    flat = jnp.dot(field.reshape(planes * size_y, size_z), basis_z, precision=HIGHEST)
    return flat.reshape(planes, size_y, size_z)


def pair_average(size):
    rows = lax.broadcasted_iota(jnp.int32, (size, size // 2), 0)
    cols = lax.broadcasted_iota(jnp.int32, (size, size // 2), 1)
    return jnp.where(rows // 2 == cols, 0.5, 0.0).astype(jnp.float32)


def restrict(fields):
    count, planes, size_y, size_z = fields.shape
    pairs = fields.reshape(count, planes // 2, 2, size_y, size_z)
    summed = (pairs[:, :, 0] + pairs[:, :, 1]) * 0.5
    flat = jnp.dot(summed.reshape(-1, size_z), pair_average(size_z), precision=HIGHEST)
    field = flat.reshape(count, planes // 2, size_y, size_z // 2)
    return jnp.einsum("ya,kpyz->kpaz", pair_average(size_y), field, precision=HIGHEST)


def fetch(value, offset, back):
    count = lax.axis_size("space")
    if back == 0:
        pairs = [((target + offset) % count, target) for target in range(count)]
        return lax.ppermute(value, "space", pairs)
    slices = lax.axis_size("tm")
    pairs = [
        ((slot - back) * count + (target + offset) % count, slot * count + target)
        for slot in range(back, slices)
        for target in range(count)
    ]
    return lax.ppermute(value, ("tm", "space"), pairs)


def cover(low, high, have, local, allowed):
    plan = []
    at = low
    while at < high:
        best = None
        for offset in allowed:
            first = offset * local - have[0]
            last = offset * local + local + have[1]
            if first <= at < last and (best is None or last > best[2]):
                best = (offset, first, last)
        if best is None:
            offset = (at + have[0]) // local
            best = (offset, offset * local - have[0], offset * local + local + have[1])
        upto = min(best[2], high)
        plan.append((best[0], at - best[1], upto - best[1]))
        at = upto
    return plan


def gather_bands(items, back=0):
    local = items[0][0].shape[0] - items[0][1][0] - items[0][1][1]
    allowed = [0] if back == 0 else []
    plans = []
    for band, have, want in items:
        plan = cover(-want[0], local + want[1], have, local, allowed)
        for offset, _, _ in plan:
            if offset not in allowed:
                allowed.append(offset)
        plans.append(plan)
    by_offset = {}
    for i, plan in enumerate(plans):
        for j, (offset, first, last) in enumerate(plan):
            by_offset.setdefault(offset, []).append((i, j, first, last))
    got = {}
    for offset, entries in by_offset.items():
        parts = [items[i][0][first:last] for i, j, first, last in entries]
        if offset == 0 and back == 0:
            for (i, j, first, last), part in zip(entries, parts):
                got[(i, j)] = part
            continue
        moved = fetch(jnp.concatenate(parts, axis=0), offset, back)
        at = 0
        for i, j, first, last in entries:
            got[(i, j)] = moved[at:at + last - first]
            at += last - first
    return [
        jnp.concatenate([got[(i, j)] for j in range(len(plan))], axis=0)
        for i, plan in enumerate(plans)
    ]


def coarse_rate(ext):
    mid = ext[1:-1]
    lap = ext[2:] + ext[:-2]
    lap = lap + jnp.roll(mid, -1, 1) + jnp.roll(mid, 1, 1)
    lap = lap + jnp.roll(mid, -1, 2) + jnp.roll(mid, 1, 2)
    return EPS2 * ((lap - 6.0 * mid) * 0.25) + react(mid)


def spread(values, following, axis):
    middle = 0.5 * (values + following)
    both = jnp.stack([values, middle], axis=axis + 1)
    shape = list(values.shape)
    shape[axis] = shape[axis] * 2
    return both.reshape(shape)


def refine(stacked):
    matrix_y = interp_matrix(stacked.shape[2])
    matrix_z = interp_matrix(stacked.shape[3])
    both = jnp.einsum("kayc,zc->kayz", stacked, matrix_z, precision=HIGHEST)
    both = jnp.einsum("Yy,kayz->kaYz", matrix_y, both, precision=HIGHEST)
    planes = stacked.shape[1] - 1
    return spread(both[:, :planes], both[:, 1:], 1)


def coarse_sweep(start, rates, sums):
    first = start[1:-1] + 0.25 * (coarse_rate(start) - rates[0]) + sums[0]
    second = first[1:-1] + 0.25 * (coarse_rate(first) - rates[1]) + sums[1]
    return (first[1:-1], second)


def on_device(fine_nodes, fine_implicit):
    nodes = fine_nodes[0]
    implicit = fine_implicit[0]
    planes, size_y, size_z = (nodes.shape[1], nodes.shape[2], nodes.shape[3])
    devices = lax.axis_size("space")
    size_x = planes * devices
    local_y = size_y // devices
    basis_x = real_basis(size_x)
    basis_y = real_basis(size_y)
    basis_z = real_basis(size_z)
    columns = lax.axis_index("space") * local_y + lax.iota(jnp.int32, local_y)
    lam = wave_square(lax.iota(jnp.int32, size_x), size_x)[:, None, None]
    lam = lam + wave_square(columns, size_y)[None, :, None]
    lam = lam + wave_square(lax.iota(jnp.int32, size_z), size_z)[None, None, :]
    factor = 1.0 / (1.0 + 0.5 * lam)
    explicit_old = react(nodes)
    rates_old = explicit_old + implicit
    values = [nodes[0]]
    terms = [implicit[0]]
    for m in range(2):
        w = WEIGHTS[m]
        quad = 0.5 * (w[0] * rates_old[0] + w[1] * rates_old[1] + w[2] * rates_old[2])
        rhs = (
            values[m] + 0.25 * (react(values[m]) - explicit_old[m]) - 0.25 * implicit[m + 1] + quad
        )
        solved = spectral_solve(rhs, basis_x, basis_y, basis_z, factor)
        values.append(solved)
        terms.append((solved - rhs) * 4.0)
    fresh = jnp.stack(values)
    rates_new = react(fresh) + jnp.stack(terms)
    sums = [0.5 * (w[0] * rates_new[0] + w[1] * rates_new[1] + w[2] * rates_new[2]) for w in WEIGHTS]
    coarse = restrict(jnp.stack([values[0], values[1], values[2], sums[0], sums[1]]))
    slot = lax.axis_index("tm")
    slices = lax.axis_size("tm")
    local = planes // 2
    near = gather_bands(
        [(coarse[0], (0, 0), (1, 1)), (coarse[1], (0, 0), (1, 1)), (coarse[3], (0, 0), (1, 1)),
         (coarse[4], (0, 0), (1, 1)), (coarse[2], (0, 0), (0, 1))]
    )
    coarse_two = near[4]
    wide = gather_bands(
        [(near[0], (1, 1), (4, 3)), (near[1], (1, 1), (3, 2)), (near[2], (1, 1), (3, 2)),
         (near[3], (1, 1), (2, 1))]
    )
    packed = coarse_two.reshape(-1, size_z)
    packed = jnp.pad(packed, ((0, size_y - packed.shape[0] % size_y), (0, 0)))
    packed = fetch(jnp.concatenate([values[2], packed.reshape(-1, size_y, size_z)]), 0, 1)
    packed, wide = lax.optimization_barrier((packed, wide))
    previous_two = packed[:planes]
    previous_coarse_two = packed[planes:].reshape(-1, size_z)[: coarse_two.size // size_z]
    previous_coarse_two = previous_coarse_two.reshape(coarse_two.shape)
    start_c = wide[0]
    rates_c = (coarse_rate(start_c), coarse_rate(wide[1]))
    sums_c = (wide[2], wide[3])
    coarse_one = wide[1][3:4 + local]
    start = start_c
    for section in range(slices - 1):
        first, second = coarse_sweep(start, rates_c, sums_c)
        received = gather_bands([(second, (2, 1), (4, 3))], back=1)[0]
        start = jnp.where(slot == 0, start_c, received)
    first, second = coarse_sweep(start, rates_c, sums_c)
    delta = jnp.stack(
        [first[2:3 + local] - coarse_one, second[2:3 + local] - coarse_two,
         start[4:5 + local] - previous_coarse_two]
    )
    corr = refine(delta)
    fixed_one = values[1] + corr[0]
    fixed_two = values[2] + corr[1]
    head = jnp.where(slot == 0, nodes[0], previous_two + corr[2])
    return (jnp.stack([head, fixed_one, fixed_two])[None], jnp.stack([terms[1], terms[2]])[None])


def solution(mesh):
    return jax.shard_map(
        on_device,
        mesh=mesh,
        in_specs=(P("tm", None, "space", None, None), P("tm", None, "space", None, None)),
        out_specs=(P("tm", None, "space", None, None), P("tm", None, "space", None, None)),
        check_vma=False,
    )
```

```python
import math

import jax
import jax.numpy as jnp
from jax import lax
from jax.sharding import PartitionSpec as P

WEIGHTS = ((5.0 / 24.0, 1.0 / 3.0, -1.0 / 24.0), (-1.0 / 24.0, 1.0 / 3.0, 5.0 / 24.0))
EPS2 = 2.0
HIGHEST = lax.Precision.HIGHEST


def react(u):
    return u - u * u * u


def real_basis(size):
    rows = lax.broadcasted_iota(jnp.int32, (size, size), 0)
    cells = lax.broadcasted_iota(jnp.int32, (size, size), 1)
    half = size // 2
    freq = jnp.where(rows <= half, rows, rows - half)
    phase = (freq * cells % size).astype(jnp.float32) * (2.0 * math.pi / size)
    scale = jnp.where((rows == 0) | (rows == half), 1.0 / math.sqrt(size), math.sqrt(2.0 / size))
    return jnp.where(rows <= half, jnp.cos(phase), jnp.sin(phase)) * scale


def wave_square(index, size):
    half = size // 2
    freq = jnp.where(index <= half, index, index - half).astype(jnp.float32)
    kappa = freq * (2.0 * math.pi / size)
    return kappa * kappa


def interp_matrix(size):
    fine_rows = lax.broadcasted_iota(jnp.int32, (2 * size, size), 0)
    coarse_cols = lax.broadcasted_iota(jnp.int32, (2 * size, size), 1)
    base = fine_rows // 2
    odd = fine_rows % 2
    take_base = jnp.where(coarse_cols == base, jnp.where(odd == 0, 1.0, 0.5), 0.0)
    take_next = jnp.where((odd == 1) & (coarse_cols == (base + 1) % size), 0.5, 0.0)
    return (take_base + take_next).astype(jnp.float32)


def spectral_solve(rhs, basis_x, basis_y, basis_z, factor):
    planes, size_y, size_z = rhs.shape
    flat = jnp.dot(rhs.reshape(planes * size_y, size_z), basis_z.T, precision=HIGHEST)
    field = flat.reshape(planes, size_y, size_z)
    field = jnp.einsum("ky,xyz->kxz", basis_y, field, precision=HIGHEST)
    field = lax.all_to_all(field, "space", split_axis=0, concat_axis=1, tiled=True)
    field = jnp.einsum("kx,yxz->kyz", basis_x, field, precision=HIGHEST) * factor
    field = jnp.einsum("kx,kyz->xyz", basis_x, field, precision=HIGHEST)
    field = lax.all_to_all(field, "space", split_axis=0, concat_axis=1, tiled=True)
    field = jnp.matmul(basis_y.T, field, precision=HIGHEST)
    flat = jnp.dot(field.reshape(planes * size_y, size_z), basis_z, precision=HIGHEST)
    return flat.reshape(planes, size_y, size_z)


def pair_average(size):
    rows = lax.broadcasted_iota(jnp.int32, (size, size // 2), 0)
    cols = lax.broadcasted_iota(jnp.int32, (size, size // 2), 1)
    return jnp.where(rows // 2 == cols, 0.5, 0.0).astype(jnp.float32)


def restrict(fields):
    count, planes, size_y, size_z = fields.shape
    pairs = fields.reshape(count, planes // 2, 2, size_y, size_z)
    summed = (pairs[:, :, 0] + pairs[:, :, 1]) * 0.5
    flat = jnp.dot(summed.reshape(-1, size_z), pair_average(size_z), precision=HIGHEST)
    field = flat.reshape(count, planes // 2, size_y, size_z // 2)
    return jnp.einsum("ya,kpyz->kpaz", pair_average(size_y), field, precision=HIGHEST)


def fetch(value, offset, back):
    count = lax.axis_size("space")
    if back == 0:
        pairs = [((target + offset) % count, target) for target in range(count)]
        return lax.ppermute(value, "space", pairs)
    slices = lax.axis_size("tm")
    pairs = [
        ((slot - back) * count + (target + offset) % count, slot * count + target)
        for slot in range(back, slices)
        for target in range(count)
    ]
    return lax.ppermute(value, ("tm", "space"), pairs)


def cover(low, high, have, local, allowed):
    plan = []
    at = low
    while at < high:
        best = None
        for offset in allowed:
            first = offset * local - have[0]
            last = offset * local + local + have[1]
            if first <= at < last and (best is None or last > best[2]):
                best = (offset, first, last)
        if best is None:
            offset = (at + have[0]) // local
            best = (offset, offset * local - have[0], offset * local + local + have[1])
        upto = min(best[2], high)
        plan.append((best[0], at - best[1], upto - best[1]))
        at = upto
    return plan


def gather_bands(items, back=0):
    local = items[0][0].shape[0] - items[0][1][0] - items[0][1][1]
    allowed = [0] if back == 0 else []
    plans = []
    for band, have, want in items:
        plan = cover(-want[0], local + want[1], have, local, allowed)
        for offset, _, _ in plan:
            if offset not in allowed:
                allowed.append(offset)
        plans.append(plan)
    by_offset = {}
    for i, plan in enumerate(plans):
        for j, (offset, first, last) in enumerate(plan):
            by_offset.setdefault(offset, []).append((i, j, first, last))
    got = {}
    for offset, entries in by_offset.items():
        parts = [items[i][0][first:last] for i, j, first, last in entries]
        if offset == 0 and back == 0:
            for (i, j, first, last), part in zip(entries, parts):
                got[(i, j)] = part
            continue
        moved = fetch(jnp.concatenate(parts, axis=0), offset, back)
        at = 0
        for i, j, first, last in entries:
            got[(i, j)] = moved[at:at + last - first]
            at += last - first
    return [
        jnp.concatenate([got[(i, j)] for j in range(len(plan))], axis=0)
        for i, plan in enumerate(plans)
    ]


def coarse_rate(ext):
    mid = ext[1:-1]
    lap = ext[2:] + ext[:-2]
    lap = lap + jnp.roll(mid, -1, 1) + jnp.roll(mid, 1, 1)
    lap = lap + jnp.roll(mid, -1, 2) + jnp.roll(mid, 1, 2)
    return EPS2 * ((lap - 6.0 * mid) * 0.25) + react(mid)


def spread(values, following, axis):
    middle = 0.5 * (values + following)
    both = jnp.stack([values, middle], axis=axis + 1)
    shape = list(values.shape)
    shape[axis] = shape[axis] * 2
    return both.reshape(shape)


def refine(stacked):
    matrix_y = interp_matrix(stacked.shape[2])
    matrix_z = interp_matrix(stacked.shape[3])
    both = jnp.einsum("kayc,zc->kayz", stacked, matrix_z, precision=HIGHEST)
    both = jnp.einsum("Yy,kayz->kaYz", matrix_y, both, precision=HIGHEST)
    planes = stacked.shape[1] - 1
    return spread(both[:, :planes], both[:, 1:], 1)


def coarse_sweep(start, rates, sums):
    first = start[1:-1] + 0.25 * (coarse_rate(start) - rates[0]) + sums[0]
    second = first[1:-1] + 0.25 * (coarse_rate(first) - rates[1]) + sums[1]
    return (first[1:-1], second)


def on_device(fine_nodes, fine_implicit):
    nodes = fine_nodes[0]
    implicit = fine_implicit[0]
    planes, size_y, size_z = (nodes.shape[1], nodes.shape[2], nodes.shape[3])
    devices = lax.axis_size("space")
    size_x = planes * devices
    local_y = size_y // devices
    basis_x = real_basis(size_x)
    basis_y = real_basis(size_y)
    basis_z = real_basis(size_z)
    columns = lax.axis_index("space") * local_y + lax.iota(jnp.int32, local_y)
    lam = wave_square(lax.iota(jnp.int32, size_x), size_x)[:, None, None]
    lam = lam + wave_square(columns, size_y)[None, :, None]
    lam = lam + wave_square(lax.iota(jnp.int32, size_z), size_z)[None, None, :]
    factor = 1.0 / (1.0 + 0.5 * lam)
    explicit_old = react(nodes)
    rates_old = explicit_old + implicit
    values = [nodes[0]]
    terms = [implicit[0]]
    for m in range(2):
        w = WEIGHTS[m]
        quad = 0.5 * (w[0] * rates_old[0] + w[1] * rates_old[1] + w[2] * rates_old[2])
        rhs = (
            values[m] + 0.25 * (react(values[m]) - explicit_old[m]) - 0.25 * implicit[m + 1] + quad
        )
        solved = spectral_solve(rhs, basis_x, basis_y, basis_z, factor)
        values.append(solved)
        terms.append((solved - rhs) * 4.0)
    fresh = jnp.stack(values)
    rates_new = react(fresh) + jnp.stack(terms)
    sums = [0.5 * (w[0] * rates_new[0] + w[1] * rates_new[1] + w[2] * rates_new[2]) for w in WEIGHTS]
    coarse = restrict(jnp.stack([values[0], values[1], values[2], sums[0], sums[1]]))
    slot = lax.axis_index("tm")
    slices = lax.axis_size("tm")
    local = planes // 2
    wide = gather_bands(
        [(coarse[0], (0, 0), (4, 3)), (coarse[1], (0, 0), (3, 2)), (coarse[3], (0, 0), (3, 2)),
         (coarse[4], (0, 0), (2, 1)), (coarse[2], (0, 0), (2, 1))]
    )
    previous_two = fetch(values[2], 0, 1)
    previous_two, wide = lax.optimization_barrier((previous_two, wide))
    start_c = wide[0]
    rates_c = (coarse_rate(start_c), coarse_rate(wide[1]))
    sums_c = (wide[2], wide[3])
    coarse_one = wide[1][3:4 + local]
    coarse_two = wide[4][2:3 + local]
    start = start_c
    previous_coarse_two = None
    for section in range(slices - 1):
        first, second = coarse_sweep(start, rates_c, sums_c)
        items = [(second, (2, 1), (4, 3))]
        if previous_coarse_two is None:
            items.append((wide[4], (2, 1), (0, 1)))
        received = gather_bands(items, back=1)
        if previous_coarse_two is None:
            previous_coarse_two = received[1]
        start = jnp.where(slot == 0, start_c, received[0])
    first, second = coarse_sweep(start, rates_c, sums_c)
    delta = jnp.stack(
        [first[2:3 + local] - coarse_one, second[2:3 + local] - coarse_two,
         start[4:5 + local] - previous_coarse_two]
    )
    corr = refine(delta)
    fixed_one = values[1] + corr[0]
    fixed_two = values[2] + corr[1]
    head = jnp.where(slot == 0, nodes[0], previous_two + corr[2])
    return (jnp.stack([head, fixed_one, fixed_two])[None], jnp.stack([terms[1], terms[2]])[None])


def solution(mesh):
    return jax.shard_map(
        on_device,
        mesh=mesh,
        in_specs=(P("tm", None, "space", None, None), P("tm", None, "space", None, None)),
        out_specs=(P("tm", None, "space", None, None), P("tm", None, "space", None, None)),
        check_vma=False,
    )
```

```python
import math

import jax
import jax.numpy as jnp
from jax import lax
from jax.sharding import PartitionSpec as P

WEIGHTS = ((5.0 / 24.0, 1.0 / 3.0, -1.0 / 24.0), (-1.0 / 24.0, 1.0 / 3.0, 5.0 / 24.0))
EPS2 = 2.0
HIGHEST = lax.Precision.HIGHEST


def react(u):
    return u - u * u * u


def real_basis(size):
    rows = lax.broadcasted_iota(jnp.int32, (size, size), 0)
    cells = lax.broadcasted_iota(jnp.int32, (size, size), 1)
    half = size // 2
    freq = jnp.where(rows <= half, rows, rows - half)
    phase = (freq * cells % size).astype(jnp.float32) * (2.0 * math.pi / size)
    scale = jnp.where((rows == 0) | (rows == half), 1.0 / math.sqrt(size), math.sqrt(2.0 / size))
    return jnp.where(rows <= half, jnp.cos(phase), jnp.sin(phase)) * scale


def wave_square(index, size):
    half = size // 2
    freq = jnp.where(index <= half, index, index - half).astype(jnp.float32)
    kappa = freq * (2.0 * math.pi / size)
    return kappa * kappa


def interp_matrix(size):
    fine_rows = lax.broadcasted_iota(jnp.int32, (2 * size, size), 0)
    coarse_cols = lax.broadcasted_iota(jnp.int32, (2 * size, size), 1)
    base = fine_rows // 2
    odd = fine_rows % 2
    take_base = jnp.where(coarse_cols == base, jnp.where(odd == 0, 1.0, 0.5), 0.0)
    take_next = jnp.where((odd == 1) & (coarse_cols == (base + 1) % size), 0.5, 0.0)
    return (take_base + take_next).astype(jnp.float32)


def spectral_solve(rhs, basis_x, basis_y, basis_z, factor):
    planes, size_y, size_z = rhs.shape
    flat = jnp.dot(rhs.reshape(planes * size_y, size_z), basis_z.T, precision=HIGHEST)
    field = flat.reshape(planes, size_y, size_z)
    field = jnp.einsum("ky,xyz->kxz", basis_y, field, precision=HIGHEST)
    field = lax.all_to_all(field, "space", split_axis=0, concat_axis=1, tiled=True)
    field = jnp.einsum("kx,yxz->kyz", basis_x, field, precision=HIGHEST) * factor
    field = jnp.einsum("kx,kyz->xyz", basis_x, field, precision=HIGHEST)
    field = lax.all_to_all(field, "space", split_axis=0, concat_axis=1, tiled=True)
    field = jnp.matmul(basis_y.T, field, precision=HIGHEST)
    flat = jnp.dot(field.reshape(planes * size_y, size_z), basis_z, precision=HIGHEST)
    return flat.reshape(planes, size_y, size_z)


def pair_average(size):
    rows = lax.broadcasted_iota(jnp.int32, (size, size // 2), 0)
    cols = lax.broadcasted_iota(jnp.int32, (size, size // 2), 1)
    return jnp.where(rows // 2 == cols, 0.5, 0.0).astype(jnp.float32)


def restrict(fields):
    count, planes, size_y, size_z = fields.shape
    pairs = fields.reshape(count, planes // 2, 2, size_y, size_z)
    summed = (pairs[:, :, 0] + pairs[:, :, 1]) * 0.5
    flat = jnp.dot(summed.reshape(-1, size_z), pair_average(size_z), precision=HIGHEST)
    field = flat.reshape(count, planes // 2, size_y, size_z // 2)
    return jnp.einsum("ya,kpyz->kpaz", pair_average(size_y), field, precision=HIGHEST)


def fetch(value, offset, back):
    count = lax.axis_size("space")
    if back == 0:
        pairs = [((target + offset) % count, target) for target in range(count)]
        return lax.ppermute(value, "space", pairs)
    slices = lax.axis_size("tm")
    pairs = [
        ((slot - back) * count + (target + offset) % count, slot * count + target)
        for slot in range(back, slices)
        for target in range(count)
    ]
    return lax.ppermute(value, ("tm", "space"), pairs)


def cover(low, high, have, local, allowed):
    plan = []
    at = low
    while at < high:
        best = None
        for offset in allowed:
            first = offset * local - have[0]
            last = offset * local + local + have[1]
            if first <= at < last and (best is None or last > best[2]):
                best = (offset, first, last)
        if best is None:
            offset = (at + have[0]) // local
            best = (offset, offset * local - have[0], offset * local + local + have[1])
        upto = min(best[2], high)
        if best[0] != 0 and 0 in allowed and at < -have[0] < upto:
            upto = -have[0]
        plan.append((best[0], at - best[1], upto - best[1]))
        at = upto
    return plan


def gather_bands(items, back=0):
    local = items[0][0].shape[0] - items[0][1][0] - items[0][1][1]
    allowed = [0] if back == 0 else []
    plans = []
    for band, have, want in items:
        plan = cover(-want[0], local + want[1], have, local, allowed)
        for offset, _, _ in plan:
            if offset not in allowed:
                allowed.append(offset)
        plans.append(plan)
    by_offset = {}
    for i, plan in enumerate(plans):
        for j, (offset, first, last) in enumerate(plan):
            by_offset.setdefault(offset, []).append((i, j, first, last))
    got = {}
    for offset, entries in by_offset.items():
        parts = [items[i][0][first:last] for i, j, first, last in entries]
        if offset == 0 and back == 0:
            for (i, j, first, last), part in zip(entries, parts):
                got[(i, j)] = part
            continue
        moved = fetch(jnp.concatenate(parts, axis=0), offset, back)
        at = 0
        for i, j, first, last in entries:
            got[(i, j)] = moved[at:at + last - first]
            at += last - first
    return [
        jnp.concatenate([got[(i, j)] for j in range(len(plan))], axis=0)
        for i, plan in enumerate(plans)
    ]


def coarse_rate(ext):
    mid = ext[1:-1]
    lap = ext[2:] + ext[:-2]
    lap = lap + jnp.roll(mid, -1, 1) + jnp.roll(mid, 1, 1)
    lap = lap + jnp.roll(mid, -1, 2) + jnp.roll(mid, 1, 2)
    return EPS2 * ((lap - 6.0 * mid) * 0.25) + react(mid)


def spread(values, following, axis):
    middle = 0.5 * (values + following)
    both = jnp.stack([values, middle], axis=axis + 1)
    shape = list(values.shape)
    shape[axis] = shape[axis] * 2
    return both.reshape(shape)


def refine(stacked):
    matrix_y = interp_matrix(stacked.shape[2])
    matrix_z = interp_matrix(stacked.shape[3])
    both = jnp.einsum("kayc,zc->kayz", stacked, matrix_z, precision=HIGHEST)
    both = jnp.einsum("Yy,kayz->kaYz", matrix_y, both, precision=HIGHEST)
    planes = stacked.shape[1] - 1
    return spread(both[:, :planes], both[:, 1:], 1)


def coarse_sweep(start, rates, sums, trim):
    inner = lambda band: band[trim:band.shape[0] - trim]
    first = start[1:-1] + 0.25 * (coarse_rate(start) - inner(rates[0])) + inner(sums[0])
    second = first[1:-1] + 0.25 * (coarse_rate(first) - inner(rates[1])) + inner(sums[1])
    return (first[1:-1], second)


def on_device(fine_nodes, fine_implicit):
    nodes = fine_nodes[0]
    implicit = fine_implicit[0]
    planes, size_y, size_z = (nodes.shape[1], nodes.shape[2], nodes.shape[3])
    devices = lax.axis_size("space")
    size_x = planes * devices
    local_y = size_y // devices
    basis_x = real_basis(size_x)
    basis_y = real_basis(size_y)
    basis_z = real_basis(size_z)
    columns = lax.axis_index("space") * local_y + lax.iota(jnp.int32, local_y)
    lam = wave_square(lax.iota(jnp.int32, size_x), size_x)[:, None, None]
    lam = lam + wave_square(columns, size_y)[None, :, None]
    lam = lam + wave_square(lax.iota(jnp.int32, size_z), size_z)[None, None, :]
    factor = 1.0 / (1.0 + 0.5 * lam)
    explicit_old = react(nodes)
    rates_old = explicit_old + implicit
    values = [nodes[0]]
    terms = [implicit[0]]
    for m in range(2):
        w = WEIGHTS[m]
        quad = 0.5 * (w[0] * rates_old[0] + w[1] * rates_old[1] + w[2] * rates_old[2])
        rhs = (
            values[m] + 0.25 * (react(values[m]) - explicit_old[m]) - 0.25 * implicit[m + 1] + quad
        )
        solved = spectral_solve(rhs, basis_x, basis_y, basis_z, factor)
        values.append(solved)
        terms.append((solved - rhs) * 4.0)
    fresh = jnp.stack(values)
    rates_new = react(fresh) + jnp.stack(terms)
    sums = [0.5 * (w[0] * rates_new[0] + w[1] * rates_new[1] + w[2] * rates_new[2]) for w in WEIGHTS]
    coarse = restrict(jnp.stack([values[0], values[1], values[2], sums[0], sums[1]]))
    slot = lax.axis_index("tm")
    slices = lax.axis_size("tm")
    local = planes // 2
    near = gather_bands(
        [(coarse[0], (0, 0), (1, 1)), (coarse[1], (0, 0), (1, 1)), (coarse[3], (0, 0), (1, 1)),
         (coarse[4], (0, 0), (1, 1)), (coarse[2], (0, 0), (0, 1))]
    )
    previous_two = fetch(values[2], 0, 1)
    previous_two, near = lax.optimization_barrier((previous_two, near))
    coarse_two = near[4]
    reach = 2 * slices
    mid = gather_bands([(band, (1, 1), (4, 4)) for band in near[:4]])
    wide = gather_bands(
        [(mid[0], (4, 4), (reach, reach + 1)), (mid[1], (4, 4), (reach - 1, reach)),
         (mid[2], (4, 4), (reach - 1, reach)), (mid[3], (4, 4), (reach - 2, reach - 1))]
    )
    start_c = wide[0]
    rates_c = (coarse_rate(start_c), coarse_rate(wide[1]))
    sums_c = (wide[2], wide[3])
    coarse_one = wide[1][reach - 1:reach + local]
    start = start_c
    previous_coarse_two = None
    for section in range(slices - 1):
        first, second = coarse_sweep(start, rates_c, sums_c, 2 * section)
        if previous_coarse_two is None:
            sent = fetch(jnp.concatenate([second, coarse_two]), 0, 1)
            received = sent[:second.shape[0]]
            previous_coarse_two = sent[second.shape[0]:]
        else:
            received = fetch(second, 0, 1)
        trim = 2 * (section + 1)
        start = jnp.where(slot == 0, start_c[trim:start_c.shape[0] - trim], received)
    first, second = coarse_sweep(start, rates_c, sums_c, 2 * (slices - 1))
    delta = jnp.stack([first - coarse_one, second - coarse_two, start[2:3 + local] - previous_coarse_two])
    corr = refine(delta)
    fixed_one = values[1] + corr[0]
    fixed_two = values[2] + corr[1]
    head = jnp.where(slot == 0, nodes[0], previous_two + corr[2])
    return (jnp.stack([head, fixed_one, fixed_two])[None], jnp.stack([terms[1], terms[2]])[None])


def solution(mesh):
    return jax.shard_map(
        on_device,
        mesh=mesh,
        in_specs=(P("tm", None, "space", None, None), P("tm", None, "space", None, None)),
        out_specs=(P("tm", None, "space", None, None), P("tm", None, "space", None, None)),
        check_vma=False,
    )
```

```python
import math

import jax
import jax.numpy as jnp
from jax import lax
from jax.sharding import PartitionSpec as P

WEIGHTS = ((5.0 / 24.0, 1.0 / 3.0, -1.0 / 24.0), (-1.0 / 24.0, 1.0 / 3.0, 5.0 / 24.0))
EPS2 = 2.0
HIGHEST = lax.Precision.HIGHEST
TRANSFORM = lax.Precision.HIGH


def react(u):
    return u - u * u * u


def real_basis(size):
    rows = lax.broadcasted_iota(jnp.int32, (size, size), 0)
    cells = lax.broadcasted_iota(jnp.int32, (size, size), 1)
    half = size // 2
    freq = jnp.where(rows <= half, rows, rows - half)
    phase = (freq * cells % size).astype(jnp.float32) * (2.0 * math.pi / size)
    scale = jnp.where((rows == 0) | (rows == half), 1.0 / math.sqrt(size), math.sqrt(2.0 / size))
    return jnp.where(rows <= half, jnp.cos(phase), jnp.sin(phase)) * scale


def wave_square(index, size):
    half = size // 2
    freq = jnp.where(index <= half, index, index - half).astype(jnp.float32)
    kappa = freq * (2.0 * math.pi / size)
    return kappa * kappa


def interp_matrix(size):
    fine_rows = lax.broadcasted_iota(jnp.int32, (2 * size, size), 0)
    coarse_cols = lax.broadcasted_iota(jnp.int32, (2 * size, size), 1)
    base = fine_rows // 2
    odd = fine_rows % 2
    take_base = jnp.where(coarse_cols == base, jnp.where(odd == 0, 1.0, 0.5), 0.0)
    take_next = jnp.where((odd == 1) & (coarse_cols == (base + 1) % size), 0.5, 0.0)
    return (take_base + take_next).astype(jnp.float32)


def spectral_solve(rhs, basis_x, basis_y, basis_z, factor):
    planes, size_y, size_z = rhs.shape
    flat = jnp.dot(rhs.reshape(planes * size_y, size_z), basis_z.T, precision=TRANSFORM)
    field = flat.reshape(planes, size_y, size_z)
    field = jnp.einsum("ky,xyz->kxz", basis_y, field, precision=TRANSFORM)
    field = lax.all_to_all(field, "space", split_axis=0, concat_axis=1, tiled=True)
    field = jnp.einsum("kx,yxz->kyz", basis_x, field, precision=TRANSFORM) * factor
    field = jnp.einsum("kx,kyz->xyz", basis_x, field, precision=TRANSFORM)
    field = lax.all_to_all(field, "space", split_axis=0, concat_axis=1, tiled=True)
    field = jnp.matmul(basis_y.T, field, precision=TRANSFORM)
    flat = jnp.dot(field.reshape(planes * size_y, size_z), basis_z, precision=TRANSFORM)
    return flat.reshape(planes, size_y, size_z)


def pair_average(size):
    rows = lax.broadcasted_iota(jnp.int32, (size, size // 2), 0)
    cols = lax.broadcasted_iota(jnp.int32, (size, size // 2), 1)
    return jnp.where(rows // 2 == cols, 0.5, 0.0).astype(jnp.float32)


def restrict(fields):
    count, planes, size_y, size_z = fields.shape
    pairs = fields.reshape(count, planes // 2, 2, size_y, size_z)
    summed = (pairs[:, :, 0] + pairs[:, :, 1]) * 0.5
    flat = jnp.dot(summed.reshape(-1, size_z), pair_average(size_z), precision=HIGHEST)
    field = flat.reshape(count, planes // 2, size_y, size_z // 2)
    return jnp.einsum("ya,kpyz->kpaz", pair_average(size_y), field, precision=HIGHEST)


def fetch(value, offset, back):
    count = lax.axis_size("space")
    if back == 0:
        pairs = [((target + offset) % count, target) for target in range(count)]
        return lax.ppermute(value, "space", pairs)
    slices = lax.axis_size("tm")
    pairs = [
        ((slot - back) * count + (target + offset) % count, slot * count + target)
        for slot in range(back, slices)
        for target in range(count)
    ]
    return lax.ppermute(value, ("tm", "space"), pairs)


def cover(low, high, have, local, allowed):
    plan = []
    at = low
    while at < high:
        best = None
        for offset in allowed:
            first = offset * local - have[0]
            last = offset * local + local + have[1]
            if first <= at < last and (best is None or last > best[2]):
                best = (offset, first, last)
        if best is None:
            offset = (at + have[0]) // local
            best = (offset, offset * local - have[0], offset * local + local + have[1])
        upto = min(best[2], high)
        plan.append((best[0], at - best[1], upto - best[1]))
        at = upto
    return plan


def gather_bands(items, back=0):
    local = items[0][0].shape[0] - items[0][1][0] - items[0][1][1]
    allowed = [0] if back == 0 else []
    plans = []
    for band, have, want in items:
        plan = cover(-want[0], local + want[1], have, local, allowed)
        for offset, _, _ in plan:
            if offset not in allowed:
                allowed.append(offset)
        plans.append(plan)
    by_offset = {}
    for i, plan in enumerate(plans):
        for j, (offset, first, last) in enumerate(plan):
            by_offset.setdefault(offset, []).append((i, j, first, last))
    got = {}
    for offset, entries in by_offset.items():
        parts = [items[i][0][first:last] for i, j, first, last in entries]
        if offset == 0 and back == 0:
            for (i, j, first, last), part in zip(entries, parts):
                got[(i, j)] = part
            continue
        moved = fetch(jnp.concatenate(parts, axis=0), offset, back)
        at = 0
        for i, j, first, last in entries:
            got[(i, j)] = moved[at:at + last - first]
            at += last - first
    return [
        jnp.concatenate([got[(i, j)] for j in range(len(plan))], axis=0)
        for i, plan in enumerate(plans)
    ]


def coarse_rate(ext):
    mid = ext[1:-1]
    lap = ext[2:] + ext[:-2]
    lap = lap + jnp.roll(mid, -1, 1) + jnp.roll(mid, 1, 1)
    lap = lap + jnp.roll(mid, -1, 2) + jnp.roll(mid, 1, 2)
    return EPS2 * ((lap - 6.0 * mid) * 0.25) + react(mid)


def spread(values, following, axis):
    middle = 0.5 * (values + following)
    both = jnp.stack([values, middle], axis=axis + 1)
    shape = list(values.shape)
    shape[axis] = shape[axis] * 2
    return both.reshape(shape)


def refine(stacked):
    matrix_y = interp_matrix(stacked.shape[2])
    matrix_z = interp_matrix(stacked.shape[3])
    both = jnp.einsum("kayc,zc->kayz", stacked, matrix_z, precision=HIGHEST)
    both = jnp.einsum("Yy,kayz->kaYz", matrix_y, both, precision=HIGHEST)
    planes = stacked.shape[1] - 1
    return spread(both[:, :planes], both[:, 1:], 1)


def coarse_sweep(start, rates, sums):
    first = start[1:-1] + 0.25 * (coarse_rate(start) - rates[0]) + sums[0]
    second = first[1:-1] + 0.25 * (coarse_rate(first) - rates[1]) + sums[1]
    return (first[1:-1], second)


def on_device(fine_nodes, fine_implicit):
    nodes = fine_nodes[0]
    implicit = fine_implicit[0]
    planes, size_y, size_z = (nodes.shape[1], nodes.shape[2], nodes.shape[3])
    devices = lax.axis_size("space")
    size_x = planes * devices
    local_y = size_y // devices
    basis_x = real_basis(size_x)
    basis_y = real_basis(size_y)
    basis_z = real_basis(size_z)
    columns = lax.axis_index("space") * local_y + lax.iota(jnp.int32, local_y)
    lam = wave_square(lax.iota(jnp.int32, size_x), size_x)[:, None, None]
    lam = lam + wave_square(columns, size_y)[None, :, None]
    lam = lam + wave_square(lax.iota(jnp.int32, size_z), size_z)[None, None, :]
    factor = 1.0 / (1.0 + 0.5 * lam)
    explicit_old = react(nodes)
    rates_old = explicit_old + implicit
    values = [nodes[0]]
    terms = [implicit[0]]
    for m in range(2):
        w = WEIGHTS[m]
        quad = 0.5 * (w[0] * rates_old[0] + w[1] * rates_old[1] + w[2] * rates_old[2])
        rhs = (
            values[m] + 0.25 * (react(values[m]) - explicit_old[m]) - 0.25 * implicit[m + 1] + quad
        )
        solved = spectral_solve(rhs, basis_x, basis_y, basis_z, factor)
        values.append(solved)
        terms.append((solved - rhs) * 4.0)
    fresh = jnp.stack(values)
    rates_new = react(fresh) + jnp.stack(terms)
    sums = [0.5 * (w[0] * rates_new[0] + w[1] * rates_new[1] + w[2] * rates_new[2]) for w in WEIGHTS]
    coarse = restrict(jnp.stack([values[0], values[1], values[2], sums[0], sums[1]]))
    slot = lax.axis_index("tm")
    slices = lax.axis_size("tm")
    local = planes // 2
    near = gather_bands(
        [(coarse[0], (0, 0), (1, 1)), (coarse[1], (0, 0), (1, 1)), (coarse[3], (0, 0), (1, 1)),
         (coarse[4], (0, 0), (1, 1)), (coarse[2], (0, 0), (0, 1))]
    )
    previous_two = fetch(values[2], 0, 1)
    previous_two, near = lax.optimization_barrier((previous_two, near))
    coarse_two = near[4]
    wide = gather_bands(
        [(near[0], (1, 1), (4, 3)), (near[1], (1, 1), (3, 2)), (near[2], (1, 1), (3, 2)),
         (near[3], (1, 1), (2, 1))]
    )
    previous_coarse_two = fetch(coarse_two, 0, 1)
    previous_coarse_two, wide = lax.optimization_barrier((previous_coarse_two, wide))
    start_c = wide[0]
    rates_c = (coarse_rate(start_c), coarse_rate(wide[1]))
    sums_c = (wide[2], wide[3])
    coarse_one = wide[1][3:4 + local]
    start = start_c
    for section in range(slices - 1):
        first, second = coarse_sweep(start, rates_c, sums_c)
        received = gather_bands([(second, (2, 1), (4, 3))], back=1)[0]
        start = jnp.where(slot == 0, start_c, received)
    first, second = coarse_sweep(start, rates_c, sums_c)
    delta = jnp.stack(
        [first[2:3 + local] - coarse_one, second[2:3 + local] - coarse_two,
         start[4:5 + local] - previous_coarse_two]
    )
    corr = refine(delta)
    fixed_one = values[1] + corr[0]
    fixed_two = values[2] + corr[1]
    head = jnp.where(slot == 0, nodes[0], previous_two + corr[2])
    return (jnp.stack([head, fixed_one, fixed_two])[None], jnp.stack([terms[1], terms[2]])[None])


def solution(mesh):
    return jax.shard_map(
        on_device,
        mesh=mesh,
        in_specs=(P("tm", None, "space", None, None), P("tm", None, "space", None, None)),
        out_specs=(P("tm", None, "space", None, None), P("tm", None, "space", None, None)),
        check_vma=False,
    )
```

```python
import math

import jax
import jax.numpy as jnp
from jax import lax
from jax.sharding import PartitionSpec as P

WEIGHTS = ((5.0 / 24.0, 1.0 / 3.0, -1.0 / 24.0), (-1.0 / 24.0, 1.0 / 3.0, 5.0 / 24.0))
EPS2 = 2.0
HIGHEST = lax.Precision.HIGHEST
TRANSFORM = lax.Precision.HIGH


def react(u):
    return u - u * u * u


def real_basis(size):
    rows = lax.broadcasted_iota(jnp.int32, (size, size), 0)
    cells = lax.broadcasted_iota(jnp.int32, (size, size), 1)
    half = size // 2
    freq = jnp.where(rows <= half, rows, rows - half)
    phase = (freq * cells % size).astype(jnp.float32) * (2.0 * math.pi / size)
    scale = jnp.where((rows == 0) | (rows == half), 1.0 / math.sqrt(size), math.sqrt(2.0 / size))
    return jnp.where(rows <= half, jnp.cos(phase), jnp.sin(phase)) * scale


def wave_square(index, size):
    half = size // 2
    freq = jnp.where(index <= half, index, index - half).astype(jnp.float32)
    kappa = freq * (2.0 * math.pi / size)
    return kappa * kappa


def interp_matrix(size):
    fine_rows = lax.broadcasted_iota(jnp.int32, (2 * size, size), 0)
    coarse_cols = lax.broadcasted_iota(jnp.int32, (2 * size, size), 1)
    base = fine_rows // 2
    odd = fine_rows % 2
    take_base = jnp.where(coarse_cols == base, jnp.where(odd == 0, 1.0, 0.5), 0.0)
    take_next = jnp.where((odd == 1) & (coarse_cols == (base + 1) % size), 0.5, 0.0)
    return (take_base + take_next).astype(jnp.float32)


def spectral_solve(rhs, basis_x, basis_y, basis_z, factor):
    planes, size_y, size_z = rhs.shape
    flat = jnp.dot(rhs.reshape(planes * size_y, size_z), basis_z.T, precision=TRANSFORM)
    field = flat.reshape(planes, size_y, size_z)
    field = jnp.einsum("ky,xyz->kxz", basis_y, field, precision=TRANSFORM)
    field = lax.all_to_all(field, "space", split_axis=0, concat_axis=1, tiled=True)
    field = jnp.einsum("kx,yxz->kyz", basis_x, field, precision=TRANSFORM) * factor
    field = jnp.einsum("kx,kyz->xyz", basis_x, field, precision=TRANSFORM)
    field = lax.all_to_all(field, "space", split_axis=0, concat_axis=1, tiled=True)
    field = jnp.matmul(basis_y.T, field, precision=TRANSFORM)
    flat = jnp.dot(field.reshape(planes * size_y, size_z), basis_z, precision=TRANSFORM)
    return flat.reshape(planes, size_y, size_z)


def pair_average(size):
    rows = lax.broadcasted_iota(jnp.int32, (size, size // 2), 0)
    cols = lax.broadcasted_iota(jnp.int32, (size, size // 2), 1)
    return jnp.where(rows // 2 == cols, 0.5, 0.0).astype(jnp.float32)


def restrict(fields):
    count, planes, size_y, size_z = fields.shape
    pairs = fields.reshape(count, planes // 2, 2, size_y, size_z)
    summed = (pairs[:, :, 0] + pairs[:, :, 1]) * 0.5
    flat = jnp.dot(summed.reshape(-1, size_z), pair_average(size_z), precision=HIGHEST)
    field = flat.reshape(count, planes // 2, size_y, size_z // 2)
    return jnp.einsum("ya,kpyz->kpaz", pair_average(size_y), field, precision=HIGHEST)


def fetch(value, offset, back):
    count = lax.axis_size("space")
    if back == 0:
        pairs = [((target + offset) % count, target) for target in range(count)]
        return lax.ppermute(value, "space", pairs)
    slices = lax.axis_size("tm")
    pairs = [
        ((slot - back) * count + (target + offset) % count, slot * count + target)
        for slot in range(back, slices)
        for target in range(count)
    ]
    return lax.ppermute(value, ("tm", "space"), pairs)


def cover(low, high, have, local, allowed):
    plan = []
    at = low
    while at < high:
        best = None
        for offset in allowed:
            first = offset * local - have[0]
            last = offset * local + local + have[1]
            if first <= at < last and (best is None or last > best[2]):
                best = (offset, first, last)
        if best is None:
            offset = (at + have[0]) // local
            best = (offset, offset * local - have[0], offset * local + local + have[1])
        upto = min(best[2], high)
        plan.append((best[0], at - best[1], upto - best[1]))
        at = upto
    return plan


def gather_bands(items, back=0):
    local = items[0][0].shape[0] - items[0][1][0] - items[0][1][1]
    allowed = [0] if back == 0 else []
    plans = []
    for band, have, want in items:
        plan = cover(-want[0], local + want[1], have, local, allowed)
        for offset, _, _ in plan:
            if offset not in allowed:
                allowed.append(offset)
        plans.append(plan)
    by_offset = {}
    for i, plan in enumerate(plans):
        for j, (offset, first, last) in enumerate(plan):
            by_offset.setdefault(offset, []).append((i, j, first, last))
    got = {}
    for offset, entries in by_offset.items():
        parts = [items[i][0][first:last] for i, j, first, last in entries]
        if offset == 0 and back == 0:
            for (i, j, first, last), part in zip(entries, parts):
                got[(i, j)] = part
            continue
        moved = fetch(jnp.concatenate(parts, axis=0), offset, back)
        at = 0
        for i, j, first, last in entries:
            got[(i, j)] = moved[at:at + last - first]
            at += last - first
    return [
        jnp.concatenate([got[(i, j)] for j in range(len(plan))], axis=0)
        for i, plan in enumerate(plans)
    ]


def coarse_rate(ext):
    mid = ext[1:-1]
    lap = ext[2:] + ext[:-2]
    lap = lap + jnp.roll(mid, -1, 1) + jnp.roll(mid, 1, 1)
    lap = lap + jnp.roll(mid, -1, 2) + jnp.roll(mid, 1, 2)
    return EPS2 * ((lap - 6.0 * mid) * 0.25) + react(mid)


def spread(values, following, axis):
    middle = 0.5 * (values + following)
    both = jnp.stack([values, middle], axis=axis + 1)
    shape = list(values.shape)
    shape[axis] = shape[axis] * 2
    return both.reshape(shape)


def refine(stacked):
    matrix_y = interp_matrix(stacked.shape[2])
    matrix_z = interp_matrix(stacked.shape[3])
    both = jnp.einsum("kayc,zc->kayz", stacked, matrix_z, precision=HIGHEST)
    both = jnp.einsum("Yy,kayz->kaYz", matrix_y, both, precision=HIGHEST)
    planes = stacked.shape[1] - 1
    return spread(both[:, :planes], both[:, 1:], 1)


def coarse_sweep(start, rates, sums):
    first = start[1:-1] + 0.25 * (coarse_rate(start) - rates[0]) + sums[0]
    second = first[1:-1] + 0.25 * (coarse_rate(first) - rates[1]) + sums[1]
    return (first[1:-1], second)


def on_device(fine_nodes, fine_implicit):
    nodes = fine_nodes[0]
    implicit = fine_implicit[0]
    planes, size_y, size_z = (nodes.shape[1], nodes.shape[2], nodes.shape[3])
    devices = lax.axis_size("space")
    size_x = planes * devices
    local_y = size_y // devices
    basis_x = real_basis(size_x)
    basis_y = real_basis(size_y)
    basis_z = real_basis(size_z)
    columns = lax.axis_index("space") * local_y + lax.iota(jnp.int32, local_y)
    lam = wave_square(lax.iota(jnp.int32, size_x), size_x)[:, None, None]
    lam = lam + wave_square(columns, size_y)[None, :, None]
    lam = lam + wave_square(lax.iota(jnp.int32, size_z), size_z)[None, None, :]
    factor = 1.0 / (1.0 + 0.5 * lam)
    explicit_old = react(nodes)
    rates_old = explicit_old + implicit
    values = [nodes[0]]
    terms = [implicit[0]]
    for m in range(2):
        w = WEIGHTS[m]
        quad = 0.5 * (w[0] * rates_old[0] + w[1] * rates_old[1] + w[2] * rates_old[2])
        rhs = (
            values[m] + 0.25 * (react(values[m]) - explicit_old[m]) - 0.25 * implicit[m + 1] + quad
        )
        solved = spectral_solve(rhs, basis_x, basis_y, basis_z, factor)
        values.append(solved)
        terms.append((solved - rhs) * 4.0)
    fresh = jnp.stack(values)
    rates_new = react(fresh) + jnp.stack(terms)
    sums = [0.5 * (w[0] * rates_new[0] + w[1] * rates_new[1] + w[2] * rates_new[2]) for w in WEIGHTS]
    coarse = restrict(jnp.stack([values[0], values[1], values[2], sums[0], sums[1]]))
    slot = lax.axis_index("tm")
    slices = lax.axis_size("tm")
    local = planes // 2
    wide = gather_bands(
        [(coarse[0], (0, 0), (2, 3)), (coarse[1], (0, 0), (1, 2)), (coarse[3], (0, 0), (1, 2)),
         (coarse[4], (0, 0), (0, 1)), (coarse[2], (0, 0), (0, 1))]
    )
    previous_two = fetch(values[2], 0, 1)
    previous_two, wide = lax.optimization_barrier((previous_two, wide))
    start_c = wide[0]
    rates_c = (coarse_rate(start_c), coarse_rate(wide[1]))
    sums_c = (wide[2], wide[3])
    coarse_one = wide[1][1:2 + local]
    coarse_two = wide[4]
    start = start_c
    previous_coarse_two = None
    for section in range(slices - 1):
        first, second = coarse_sweep(start, rates_c, sums_c)
        items = [(second, (0, 1), (2, 3))]
        if previous_coarse_two is None:
            items.append((coarse_two, (0, 1), (0, 1)))
        received = gather_bands(items, back=1)
        if previous_coarse_two is None:
            previous_coarse_two = received[1]
        start = jnp.where(slot == 0, start_c, received[0])
    first, second = coarse_sweep(start, rates_c, sums_c)
    delta = jnp.stack(
        [first - coarse_one, second - coarse_two,
         start[2:3 + local] - previous_coarse_two]
    )
    corr = refine(delta)
    fixed_one = values[1] + corr[0]
    fixed_two = values[2] + corr[1]
    head = jnp.where(slot == 0, nodes[0], previous_two + corr[2])
    return (jnp.stack([head, fixed_one, fixed_two])[None], jnp.stack([terms[1], terms[2]])[None])


def solution(mesh):
    return jax.shard_map(
        on_device,
        mesh=mesh,
        in_specs=(P("tm", None, "space", None, None), P("tm", None, "space", None, None)),
        out_specs=(P("tm", None, "space", None, None), P("tm", None, "space", None, None)),
        check_vma=False,
    )
```

```python
import math

import jax
import jax.numpy as jnp
from jax import lax
from jax.sharding import PartitionSpec as P

WEIGHTS = ((5.0 / 24.0, 1.0 / 3.0, -1.0 / 24.0), (-1.0 / 24.0, 1.0 / 3.0, 5.0 / 24.0))
EPS2 = 2.0
HIGHEST = lax.Precision.HIGHEST
TRANSFORM = lax.Precision.HIGH


def react(u):
    return u - u * u * u


def real_basis(size):
    rows = lax.broadcasted_iota(jnp.int32, (size, size), 0)
    cells = lax.broadcasted_iota(jnp.int32, (size, size), 1)
    half = size // 2
    freq = jnp.where(rows <= half, rows, rows - half)
    phase = (freq * cells % size).astype(jnp.float32) * (2.0 * math.pi / size)
    scale = jnp.where((rows == 0) | (rows == half), 1.0 / math.sqrt(size), math.sqrt(2.0 / size))
    return jnp.where(rows <= half, jnp.cos(phase), jnp.sin(phase)) * scale


def wave_square(index, size):
    half = size // 2
    freq = jnp.where(index <= half, index, index - half).astype(jnp.float32)
    kappa = freq * (2.0 * math.pi / size)
    return kappa * kappa


def interp_matrix(size):
    fine_rows = lax.broadcasted_iota(jnp.int32, (2 * size, size), 0)
    coarse_cols = lax.broadcasted_iota(jnp.int32, (2 * size, size), 1)
    base = fine_rows // 2
    odd = fine_rows % 2
    take_base = jnp.where(coarse_cols == base, jnp.where(odd == 0, 1.0, 0.5), 0.0)
    take_next = jnp.where((odd == 1) & (coarse_cols == (base + 1) % size), 0.5, 0.0)
    return (take_base + take_next).astype(jnp.float32)


def spectral_solve(rhs, basis_x, basis_y, basis_z, factor):
    planes, size_y, size_z = rhs.shape
    flat = jnp.dot(rhs.reshape(planes * size_y, size_z), basis_z.T, precision=TRANSFORM)
    field = flat.reshape(planes, size_y, size_z)
    field = jnp.einsum("ky,xyz->kxz", basis_y, field, precision=TRANSFORM)
    field = lax.all_to_all(field, "space", split_axis=0, concat_axis=1, tiled=True)
    field = jnp.einsum("kx,yxz->kyz", basis_x, field, precision=TRANSFORM) * factor
    field = jnp.einsum("kx,kyz->xyz", basis_x, field, precision=TRANSFORM)
    field = lax.all_to_all(field, "space", split_axis=0, concat_axis=1, tiled=True)
    field = jnp.matmul(basis_y.T, field, precision=TRANSFORM)
    flat = jnp.dot(field.reshape(planes * size_y, size_z), basis_z, precision=TRANSFORM)
    return flat.reshape(planes, size_y, size_z)


def pair_average(size):
    rows = lax.broadcasted_iota(jnp.int32, (size, size // 2), 0)
    cols = lax.broadcasted_iota(jnp.int32, (size, size // 2), 1)
    return jnp.where(rows // 2 == cols, 0.5, 0.0).astype(jnp.float32)


def restrict(fields):
    count, planes, size_y, size_z = fields.shape
    pairs = fields.reshape(count, planes // 2, 2, size_y, size_z)
    summed = (pairs[:, :, 0] + pairs[:, :, 1]) * 0.5
    flat = jnp.dot(summed.reshape(-1, size_z), pair_average(size_z), precision=HIGHEST)
    field = flat.reshape(count, planes // 2, size_y, size_z // 2)
    return jnp.einsum("ya,kpyz->kpaz", pair_average(size_y), field, precision=HIGHEST)


def fetch(value, offset, back):
    count = lax.axis_size("space")
    if back == 0:
        pairs = [((target + offset) % count, target) for target in range(count)]
        return lax.ppermute(value, "space", pairs)
    slices = lax.axis_size("tm")
    pairs = [
        ((slot - back) * count + (target + offset) % count, slot * count + target)
        for slot in range(back, slices)
        for target in range(count)
    ]
    return lax.ppermute(value, ("tm", "space"), pairs)


def cover(low, high, have, local, allowed):
    plan = []
    at = low
    while at < high:
        best = None
        for offset in allowed:
            first = offset * local - have[0]
            last = offset * local + local + have[1]
            if first <= at < last and (best is None or last > best[2]):
                best = (offset, first, last)
        if best is None:
            offset = (at + have[0]) // local
            best = (offset, offset * local - have[0], offset * local + local + have[1])
        upto = min(best[2], high)
        plan.append((best[0], at - best[1], upto - best[1]))
        at = upto
    return plan


def gather_bands(items, back=0):
    local = items[0][0].shape[0] - items[0][1][0] - items[0][1][1]
    allowed = [0] if back == 0 else []
    plans = []
    for band, have, want in items:
        plan = cover(-want[0], local + want[1], have, local, allowed)
        for offset, _, _ in plan:
            if offset not in allowed:
                allowed.append(offset)
        plans.append(plan)
    by_offset = {}
    for i, plan in enumerate(plans):
        for j, (offset, first, last) in enumerate(plan):
            by_offset.setdefault(offset, []).append((i, j, first, last))
    got = {}
    for offset, entries in by_offset.items():
        parts = [items[i][0][first:last] for i, j, first, last in entries]
        if offset == 0 and back == 0:
            for (i, j, first, last), part in zip(entries, parts):
                got[(i, j)] = part
            continue
        moved = fetch(jnp.concatenate(parts, axis=0), offset, back)
        at = 0
        for i, j, first, last in entries:
            got[(i, j)] = moved[at:at + last - first]
            at += last - first
    return [
        jnp.concatenate([got[(i, j)] for j in range(len(plan))], axis=0)
        for i, plan in enumerate(plans)
    ]


def coarse_rate(ext):
    mid = ext[1:-1]
    lap = ext[2:] + ext[:-2]
    lap = lap + jnp.roll(mid, -1, 1) + jnp.roll(mid, 1, 1)
    lap = lap + jnp.roll(mid, -1, 2) + jnp.roll(mid, 1, 2)
    return EPS2 * ((lap - 6.0 * mid) * 0.25) + react(mid)


def spread(values, following, axis):
    middle = 0.5 * (values + following)
    both = jnp.stack([values, middle], axis=axis + 1)
    shape = list(values.shape)
    shape[axis] = shape[axis] * 2
    return both.reshape(shape)


def refine(stacked):
    matrix_y = interp_matrix(stacked.shape[2])
    matrix_z = interp_matrix(stacked.shape[3])
    both = jnp.einsum("kayc,zc->kayz", stacked, matrix_z, precision=HIGHEST)
    both = jnp.einsum("Yy,kayz->kaYz", matrix_y, both, precision=HIGHEST)
    planes = stacked.shape[1] - 1
    return spread(both[:, :planes], both[:, 1:], 1)


def coarse_sweep(start, rates, sums):
    first = start[1:-1] + 0.25 * (coarse_rate(start) - rates[0]) + sums[0]
    second = first[1:-1] + 0.25 * (coarse_rate(first) - rates[1]) + sums[1]
    return (first[1:-1], second)


def on_device(fine_nodes, fine_implicit):
    nodes = fine_nodes[0]
    implicit = fine_implicit[0]
    planes, size_y, size_z = (nodes.shape[1], nodes.shape[2], nodes.shape[3])
    devices = lax.axis_size("space")
    size_x = planes * devices
    local_y = size_y // devices
    basis_x = real_basis(size_x)
    basis_y = real_basis(size_y)
    basis_z = real_basis(size_z)
    columns = lax.axis_index("space") * local_y + lax.iota(jnp.int32, local_y)
    lam = wave_square(lax.iota(jnp.int32, size_x), size_x)[:, None, None]
    lam = lam + wave_square(columns, size_y)[None, :, None]
    lam = lam + wave_square(lax.iota(jnp.int32, size_z), size_z)[None, None, :]
    factor = 1.0 / (1.0 + 0.5 * lam)
    explicit_old = react(nodes)
    rates_old = explicit_old + implicit
    start_c = gather_bands([(restrict(nodes[0:1])[0], (0, 0), (2, 3))])[0]
    rate_start = coarse_rate(start_c)
    values = [nodes[0]]
    terms = [implicit[0]]
    for m in range(2):
        w = WEIGHTS[m]
        quad = 0.5 * (w[0] * rates_old[0] + w[1] * rates_old[1] + w[2] * rates_old[2])
        rhs = (
            values[m] + 0.25 * (react(values[m]) - explicit_old[m]) - 0.25 * implicit[m + 1] + quad
        )
        solved = spectral_solve(rhs, basis_x, basis_y, basis_z, factor)
        values.append(solved)
        terms.append((solved - rhs) * 4.0)
    fresh = jnp.stack(values)
    rates_new = react(fresh) + jnp.stack(terms)
    sums = [0.5 * (w[0] * rates_new[0] + w[1] * rates_new[1] + w[2] * rates_new[2]) for w in WEIGHTS]
    coarse = restrict(jnp.stack([values[1], values[2], sums[0], sums[1]]))
    slot = lax.axis_index("tm")
    slices = lax.axis_size("tm")
    local = planes // 2
    wide = gather_bands(
        [(coarse[0], (0, 0), (1, 2)), (coarse[2], (0, 0), (1, 2)), (coarse[3], (0, 0), (0, 1)),
         (coarse[1], (0, 0), (0, 1))]
    )
    previous_two = fetch(values[2], 0, 1)
    previous_two, wide = lax.optimization_barrier((previous_two, wide))
    rates_c = (rate_start, coarse_rate(wide[0]))
    sums_c = (wide[1], wide[2])
    coarse_one = wide[0][1:2 + local]
    coarse_two = wide[3]
    start = start_c
    previous_coarse_two = None
    for section in range(slices - 1):
        first, second = coarse_sweep(start, rates_c, sums_c)
        items = [(second, (0, 1), (2, 3))]
        if previous_coarse_two is None:
            items.append((coarse_two, (0, 1), (0, 1)))
        received = gather_bands(items, back=1)
        if previous_coarse_two is None:
            previous_coarse_two = received[1]
        start = jnp.where(slot == 0, start_c, received[0])
    first, second = coarse_sweep(start, rates_c, sums_c)
    delta = jnp.stack(
        [first - coarse_one, second - coarse_two,
         start[2:3 + local] - previous_coarse_two]
    )
    corr = refine(delta)
    fixed_one = values[1] + corr[0]
    fixed_two = values[2] + corr[1]
    head = jnp.where(slot == 0, nodes[0], previous_two + corr[2])
    return (jnp.stack([head, fixed_one, fixed_two])[None], jnp.stack([terms[1], terms[2]])[None])


def solution(mesh):
    return jax.shard_map(
        on_device,
        mesh=mesh,
        in_specs=(P("tm", None, "space", None, None), P("tm", None, "space", None, None)),
        out_specs=(P("tm", None, "space", None, None), P("tm", None, "space", None, None)),
        check_vma=False,
    )
```

```python
import math

import jax
import jax.numpy as jnp
from jax import lax
from jax.sharding import PartitionSpec as P

WEIGHTS = ((5.0 / 24.0, 1.0 / 3.0, -1.0 / 24.0), (-1.0 / 24.0, 1.0 / 3.0, 5.0 / 24.0))
EPS2 = 2.0
HIGHEST = lax.Precision.HIGHEST
TRANSFORM = lax.Precision.HIGH


def react(u):
    return u - u * u * u


def real_basis(size):
    rows = lax.broadcasted_iota(jnp.int32, (size, size), 0)
    cells = lax.broadcasted_iota(jnp.int32, (size, size), 1)
    half = size // 2
    freq = jnp.where(rows <= half, rows, rows - half)
    phase = (freq * cells % size).astype(jnp.float32) * (2.0 * math.pi / size)
    scale = jnp.where((rows == 0) | (rows == half), 1.0 / math.sqrt(size), math.sqrt(2.0 / size))
    return jnp.where(rows <= half, jnp.cos(phase), jnp.sin(phase)) * scale


def wave_square(index, size):
    half = size // 2
    freq = jnp.where(index <= half, index, index - half).astype(jnp.float32)
    kappa = freq * (2.0 * math.pi / size)
    return kappa * kappa


def interp_matrix(size):
    fine_rows = lax.broadcasted_iota(jnp.int32, (2 * size, size), 0)
    coarse_cols = lax.broadcasted_iota(jnp.int32, (2 * size, size), 1)
    base = fine_rows // 2
    odd = fine_rows % 2
    take_base = jnp.where(coarse_cols == base, jnp.where(odd == 0, 1.0, 0.5), 0.0)
    take_next = jnp.where((odd == 1) & (coarse_cols == (base + 1) % size), 0.5, 0.0)
    return (take_base + take_next).astype(jnp.float32)


def spectral_solve(rhs, basis_x, basis_y, basis_z, factor):
    planes, size_y, size_z = rhs.shape
    flat = jnp.dot(rhs.reshape(planes * size_y, size_z), basis_z.T, precision=TRANSFORM)
    field = flat.reshape(planes, size_y, size_z)
    field = jnp.einsum("ky,xyz->kxz", basis_y, field, precision=TRANSFORM)
    field = lax.all_to_all(field, "space", split_axis=0, concat_axis=1, tiled=True)
    field = jnp.einsum("kx,yxz->kyz", basis_x, field, precision=TRANSFORM) * factor
    field = jnp.einsum("kx,kyz->xyz", basis_x, field, precision=TRANSFORM)
    field = lax.all_to_all(field, "space", split_axis=0, concat_axis=1, tiled=True)
    field = jnp.matmul(basis_y.T, field, precision=TRANSFORM)
    flat = jnp.dot(field.reshape(planes * size_y, size_z), basis_z, precision=TRANSFORM)
    return flat.reshape(planes, size_y, size_z)


def pair_average(size):
    rows = lax.broadcasted_iota(jnp.int32, (size, size // 2), 0)
    cols = lax.broadcasted_iota(jnp.int32, (size, size // 2), 1)
    return jnp.where(rows // 2 == cols, 0.5, 0.0).astype(jnp.float32)


def restrict(fields):
    count, planes, size_y, size_z = fields.shape
    pairs = fields.reshape(count, planes // 2, 2, size_y, size_z)
    summed = (pairs[:, :, 0] + pairs[:, :, 1]) * 0.5
    flat = jnp.dot(summed.reshape(-1, size_z), pair_average(size_z), precision=TRANSFORM)
    field = flat.reshape(count, planes // 2, size_y, size_z // 2)
    return jnp.einsum("ya,kpyz->kpaz", pair_average(size_y), field, precision=TRANSFORM)


def fetch(value, offset, back):
    count = lax.axis_size("space")
    if back == 0:
        pairs = [((target + offset) % count, target) for target in range(count)]
        return lax.ppermute(value, "space", pairs)
    slices = lax.axis_size("tm")
    pairs = [
        ((slot - back) * count + (target + offset) % count, slot * count + target)
        for slot in range(back, slices)
        for target in range(count)
    ]
    return lax.ppermute(value, ("tm", "space"), pairs)


def cover(low, high, have, local, allowed):
    plan = []
    at = low
    while at < high:
        best = None
        for offset in allowed:
            first = offset * local - have[0]
            last = offset * local + local + have[1]
            if first <= at < last and (best is None or last > best[2]):
                best = (offset, first, last)
        if best is None:
            offset = (at + have[0]) // local
            best = (offset, offset * local - have[0], offset * local + local + have[1])
        upto = min(best[2], high)
        plan.append((best[0], at - best[1], upto - best[1]))
        at = upto
    return plan


def gather_bands(items, back=0):
    local = items[0][0].shape[0] - items[0][1][0] - items[0][1][1]
    allowed = [0] if back == 0 else []
    plans = []
    for band, have, want in items:
        plan = cover(-want[0], local + want[1], have, local, allowed)
        for offset, _, _ in plan:
            if offset not in allowed:
                allowed.append(offset)
        plans.append(plan)
    by_offset = {}
    for i, plan in enumerate(plans):
        for j, (offset, first, last) in enumerate(plan):
            by_offset.setdefault(offset, []).append((i, j, first, last))
    got = {}
    for offset, entries in by_offset.items():
        parts = [items[i][0][first:last] for i, j, first, last in entries]
        if offset == 0 and back == 0:
            for (i, j, first, last), part in zip(entries, parts):
                got[(i, j)] = part
            continue
        moved = fetch(jnp.concatenate(parts, axis=0), offset, back)
        at = 0
        for i, j, first, last in entries:
            got[(i, j)] = moved[at:at + last - first]
            at += last - first
    return [
        jnp.concatenate([got[(i, j)] for j in range(len(plan))], axis=0)
        for i, plan in enumerate(plans)
    ]


def coarse_rate(ext):
    mid = ext[1:-1]
    lap = ext[2:] + ext[:-2]
    lap = lap + jnp.roll(mid, -1, 1) + jnp.roll(mid, 1, 1)
    lap = lap + jnp.roll(mid, -1, 2) + jnp.roll(mid, 1, 2)
    return EPS2 * ((lap - 6.0 * mid) * 0.25) + react(mid)


def spread(values, following, axis):
    middle = 0.5 * (values + following)
    both = jnp.stack([values, middle], axis=axis + 1)
    shape = list(values.shape)
    shape[axis] = shape[axis] * 2
    return both.reshape(shape)


def refine(stacked):
    matrix_y = interp_matrix(stacked.shape[2])
    matrix_z = interp_matrix(stacked.shape[3])
    both = jnp.einsum("kayc,zc->kayz", stacked, matrix_z, precision=TRANSFORM)
    both = jnp.einsum("Yy,kayz->kaYz", matrix_y, both, precision=TRANSFORM)
    planes = stacked.shape[1] - 1
    return spread(both[:, :planes], both[:, 1:], 1)


def coarse_sweep(start, rates, sums):
    first = start[1:-1] + 0.25 * (coarse_rate(start) - rates[0]) + sums[0]
    second = first[1:-1] + 0.25 * (coarse_rate(first) - rates[1]) + sums[1]
    return (first[1:-1], second)


def on_device(fine_nodes, fine_implicit):
    nodes = fine_nodes[0]
    implicit = fine_implicit[0]
    planes, size_y, size_z = (nodes.shape[1], nodes.shape[2], nodes.shape[3])
    devices = lax.axis_size("space")
    size_x = planes * devices
    local_y = size_y // devices
    basis_x = real_basis(size_x)
    basis_y = real_basis(size_y)
    basis_z = real_basis(size_z)
    columns = lax.axis_index("space") * local_y + lax.iota(jnp.int32, local_y)
    lam = wave_square(lax.iota(jnp.int32, size_x), size_x)[:, None, None]
    lam = lam + wave_square(columns, size_y)[None, :, None]
    lam = lam + wave_square(lax.iota(jnp.int32, size_z), size_z)[None, None, :]
    factor = 1.0 / (1.0 + 0.5 * lam)
    explicit_old = react(nodes)
    rates_old = explicit_old + implicit
    values = [nodes[0]]
    terms = [implicit[0]]
    for m in range(2):
        w = WEIGHTS[m]
        quad = 0.5 * (w[0] * rates_old[0] + w[1] * rates_old[1] + w[2] * rates_old[2])
        rhs = (
            values[m] + 0.25 * (react(values[m]) - explicit_old[m]) - 0.25 * implicit[m + 1] + quad
        )
        solved = spectral_solve(rhs, basis_x, basis_y, basis_z, factor)
        values.append(solved)
        terms.append((solved - rhs) * 4.0)
    fresh = jnp.stack(values)
    rates_new = react(fresh) + jnp.stack(terms)
    sums = [0.5 * (w[0] * rates_new[0] + w[1] * rates_new[1] + w[2] * rates_new[2]) for w in WEIGHTS]
    coarse = restrict(jnp.stack([values[0], values[1], values[2], sums[0], sums[1]]))
    slot = lax.axis_index("tm")
    slices = lax.axis_size("tm")
    local = planes // 2
    wide = gather_bands(
        [(coarse[0], (0, 0), (2, 3)), (coarse[1], (0, 0), (1, 2)), (coarse[3], (0, 0), (1, 2)),
         (coarse[4], (0, 0), (0, 1)), (coarse[2], (0, 0), (0, 1))]
    )
    previous_two = fetch(values[2], 0, 1)
    previous_two, wide = lax.optimization_barrier((previous_two, wide))
    start_c = wide[0]
    rates_c = (coarse_rate(start_c), coarse_rate(wide[1]))
    sums_c = (wide[2], wide[3])
    coarse_one = wide[1][1:2 + local]
    coarse_two = wide[4]
    start = start_c
    previous_coarse_two = None
    for section in range(slices - 1):
        first, second = coarse_sweep(start, rates_c, sums_c)
        items = [(second, (0, 1), (2, 3))]
        if previous_coarse_two is None:
            items.append((coarse_two, (0, 1), (0, 1)))
        received = gather_bands(items, back=1)
        if previous_coarse_two is None:
            previous_coarse_two = received[1]
        start = jnp.where(slot == 0, start_c, received[0])
    first, second = coarse_sweep(start, rates_c, sums_c)
    delta = jnp.stack(
        [first - coarse_one, second - coarse_two,
         start[2:3 + local] - previous_coarse_two]
    )
    corr = refine(delta)
    fixed_one = values[1] + corr[0]
    fixed_two = values[2] + corr[1]
    head = jnp.where(slot == 0, nodes[0], previous_two + corr[2])
    return (jnp.stack([head, fixed_one, fixed_two])[None], jnp.stack([terms[1], terms[2]])[None])


def solution(mesh):
    return jax.shard_map(
        on_device,
        mesh=mesh,
        in_specs=(P("tm", None, "space", None, None), P("tm", None, "space", None, None)),
        out_specs=(P("tm", None, "space", None, None), P("tm", None, "space", None, None)),
        check_vma=False,
    )
```

```python
import math

import jax
import jax.numpy as jnp
from jax import lax
from jax.sharding import PartitionSpec as P

WEIGHTS = ((5.0 / 24.0, 1.0 / 3.0, -1.0 / 24.0), (-1.0 / 24.0, 1.0 / 3.0, 5.0 / 24.0))
EPS2 = 2.0
HIGHEST = lax.Precision.HIGHEST
TRANSFORM = lax.Precision.HIGH


def react(u):
    return u - u * u * u


def real_basis(size):
    rows = lax.broadcasted_iota(jnp.int32, (size, size), 0)
    cells = lax.broadcasted_iota(jnp.int32, (size, size), 1)
    half = size // 2
    freq = jnp.where(rows <= half, rows, rows - half)
    phase = (freq * cells % size).astype(jnp.float32) * (2.0 * math.pi / size)
    scale = jnp.where((rows == 0) | (rows == half), 1.0 / math.sqrt(size), math.sqrt(2.0 / size))
    return jnp.where(rows <= half, jnp.cos(phase), jnp.sin(phase)) * scale


def wave_square(index, size):
    half = size // 2
    freq = jnp.where(index <= half, index, index - half).astype(jnp.float32)
    kappa = freq * (2.0 * math.pi / size)
    return kappa * kappa


def interp_matrix(size):
    fine_rows = lax.broadcasted_iota(jnp.int32, (2 * size, size), 0)
    coarse_cols = lax.broadcasted_iota(jnp.int32, (2 * size, size), 1)
    base = fine_rows // 2
    odd = fine_rows % 2
    take_base = jnp.where(coarse_cols == base, jnp.where(odd == 0, 1.0, 0.5), 0.0)
    take_next = jnp.where((odd == 1) & (coarse_cols == (base + 1) % size), 0.5, 0.0)
    return (take_base + take_next).astype(jnp.float32)


def spectral_solve(rhs, basis_x, basis_y, basis_z, factor):
    planes, size_y, size_z = rhs.shape
    flat = jnp.dot(rhs.reshape(planes * size_y, size_z), basis_z.T, precision=TRANSFORM)
    field = flat.reshape(planes, size_y, size_z)
    field = jnp.einsum("ky,xyz->kxz", basis_y, field, precision=TRANSFORM)
    field = lax.all_to_all(field, "space", split_axis=0, concat_axis=1, tiled=True)
    field = jnp.einsum("kx,yxz->kyz", basis_x, field, precision=TRANSFORM) * factor
    field = jnp.einsum("kx,kyz->xyz", basis_x, field, precision=TRANSFORM)
    field = lax.all_to_all(field, "space", split_axis=0, concat_axis=1, tiled=True)
    field = jnp.matmul(basis_y.T, field, precision=TRANSFORM)
    flat = jnp.dot(field.reshape(planes * size_y, size_z), basis_z, precision=TRANSFORM)
    return flat.reshape(planes, size_y, size_z)


def pair_average(size):
    rows = lax.broadcasted_iota(jnp.int32, (size, size // 2), 0)
    cols = lax.broadcasted_iota(jnp.int32, (size, size // 2), 1)
    return jnp.where(rows // 2 == cols, 0.5, 0.0).astype(jnp.float32)


def restrict(fields):
    count, planes, size_y, size_z = fields.shape
    pairs = fields.reshape(count, planes // 2, 2, size_y, size_z)
    summed = (pairs[:, :, 0] + pairs[:, :, 1]) * 0.5
    flat = jnp.dot(summed.reshape(-1, size_z), pair_average(size_z), precision=TRANSFORM)
    field = flat.reshape(count, planes // 2, size_y, size_z // 2)
    return jnp.einsum("ya,kpyz->kpaz", pair_average(size_y), field, precision=TRANSFORM)


def fetch(value, offset, back):
    count = lax.axis_size("space")
    if back == 0:
        pairs = [((target + offset) % count, target) for target in range(count)]
        return lax.ppermute(value, "space", pairs)
    slices = lax.axis_size("tm")
    pairs = [
        ((slot - back) * count + (target + offset) % count, slot * count + target)
        for slot in range(back, slices)
        for target in range(count)
    ]
    return lax.ppermute(value, ("tm", "space"), pairs)


def cover(low, high, have, local, allowed):
    plan = []
    at = low
    while at < high:
        best = None
        for offset in allowed:
            first = offset * local - have[0]
            last = offset * local + local + have[1]
            if first <= at < last and (best is None or last > best[2]):
                best = (offset, first, last)
        if best is None:
            offset = (at + have[0]) // local
            best = (offset, offset * local - have[0], offset * local + local + have[1])
        upto = min(best[2], high)
        plan.append((best[0], at - best[1], upto - best[1]))
        at = upto
    return plan


def gather_bands(items, back=0):
    local = items[0][0].shape[0] - items[0][1][0] - items[0][1][1]
    allowed = [0] if back == 0 else []
    plans = []
    for band, have, want in items:
        plan = cover(-want[0], local + want[1], have, local, allowed)
        for offset, _, _ in plan:
            if offset not in allowed:
                allowed.append(offset)
        plans.append(plan)
    by_offset = {}
    for i, plan in enumerate(plans):
        for j, (offset, first, last) in enumerate(plan):
            by_offset.setdefault(offset, []).append((i, j, first, last))
    got = {}
    for offset, entries in by_offset.items():
        parts = [items[i][0][first:last] for i, j, first, last in entries]
        if offset == 0 and back == 0:
            for (i, j, first, last), part in zip(entries, parts):
                got[(i, j)] = part
            continue
        moved = fetch(jnp.concatenate(parts, axis=0), offset, back)
        at = 0
        for i, j, first, last in entries:
            got[(i, j)] = moved[at:at + last - first]
            at += last - first
    return [
        jnp.concatenate([got[(i, j)] for j in range(len(plan))], axis=0)
        for i, plan in enumerate(plans)
    ]


def coarse_rate(ext):
    mid = ext[1:-1]
    lap = ext[2:] + ext[:-2]
    lap = lap + jnp.roll(mid, -1, 1) + jnp.roll(mid, 1, 1)
    lap = lap + jnp.roll(mid, -1, 2) + jnp.roll(mid, 1, 2)
    return EPS2 * ((lap - 6.0 * mid) * 0.25) + react(mid)


def spread(values, following, axis):
    middle = 0.5 * (values + following)
    both = jnp.stack([values, middle], axis=axis + 1)
    shape = list(values.shape)
    shape[axis] = shape[axis] * 2
    return both.reshape(shape)


def refine(stacked):
    matrix_y = interp_matrix(stacked.shape[2])
    matrix_z = interp_matrix(stacked.shape[3])
    both = jnp.einsum("kayc,zc->kayz", stacked, matrix_z, precision=TRANSFORM)
    both = jnp.einsum("Yy,kayz->kaYz", matrix_y, both, precision=TRANSFORM)
    planes = stacked.shape[1] - 1
    return spread(both[:, :planes], both[:, 1:], 1)


def coarse_sweep(start, rates, sums):
    first = start[1:-1] + 0.25 * (coarse_rate(start) - rates[0]) + sums[0]
    second = first[1:-1] + 0.25 * (coarse_rate(first) - rates[1]) + sums[1]
    return (first[1:-1], second)


def on_device(fine_nodes, fine_implicit):
    nodes = fine_nodes[0]
    implicit = fine_implicit[0]
    planes, size_y, size_z = (nodes.shape[1], nodes.shape[2], nodes.shape[3])
    devices = lax.axis_size("space")
    size_x = planes * devices
    local_y = size_y // devices
    basis_x = real_basis(size_x)
    basis_y = real_basis(size_y)
    basis_z = real_basis(size_z)
    columns = lax.axis_index("space") * local_y + lax.iota(jnp.int32, local_y)
    lam = wave_square(lax.iota(jnp.int32, size_x), size_x)[:, None, None]
    lam = lam + wave_square(columns, size_y)[None, :, None]
    lam = lam + wave_square(lax.iota(jnp.int32, size_z), size_z)[None, None, :]
    factor = 1.0 / (1.0 + 0.5 * lam)
    explicit_old = react(nodes)
    rates_old = explicit_old + implicit
    values = [nodes[0]]
    terms = [implicit[0]]
    for m in range(2):
        w = WEIGHTS[m]
        quad = 0.5 * (w[0] * rates_old[0] + w[1] * rates_old[1] + w[2] * rates_old[2])
        rhs = (
            values[m] + 0.25 * (react(values[m]) - explicit_old[m]) - 0.25 * implicit[m + 1] + quad
        )
        solved = spectral_solve(rhs, basis_x, basis_y, basis_z, factor)
        values.append(solved)
        terms.append((solved - rhs) * 4.0)
    rates_new = [react(values[j]) + terms[j] for j in range(3)]
    known = [0.5 * (w[0] * rates_new[0] + w[1] * rates_new[1]) for w in WEIGHTS]
    known = restrict(jnp.stack([values[0], values[1], known[0], known[1]]))
    last = [0.5 * (w[2] * rates_new[2]) for w in WEIGHTS]
    last = restrict(jnp.stack([values[2], last[0], last[1]]))
    coarse = [known[0], known[1], last[0], known[2] + last[1], known[3] + last[2]]
    slot = lax.axis_index("tm")
    slices = lax.axis_size("tm")
    local = planes // 2
    wide = gather_bands(
        [(coarse[0], (0, 0), (2, 3)), (coarse[1], (0, 0), (1, 2)), (coarse[3], (0, 0), (1, 2)),
         (coarse[4], (0, 0), (0, 1)), (coarse[2], (0, 0), (0, 1))]
    )
    previous_two = fetch(values[2], 0, 1)
    previous_two, wide = lax.optimization_barrier((previous_two, wide))
    start_c = wide[0]
    rates_c = (coarse_rate(start_c), coarse_rate(wide[1]))
    sums_c = (wide[2], wide[3])
    coarse_one = wide[1][1:2 + local]
    coarse_two = wide[4]
    start = start_c
    previous_coarse_two = None
    for section in range(slices - 1):
        first, second = coarse_sweep(start, rates_c, sums_c)
        items = [(second, (0, 1), (2, 3))]
        if previous_coarse_two is None:
            items.append((coarse_two, (0, 1), (0, 1)))
        received = gather_bands(items, back=1)
        if previous_coarse_two is None:
            previous_coarse_two = received[1]
        start = jnp.where(slot == 0, start_c, received[0])
    first, second = coarse_sweep(start, rates_c, sums_c)
    delta = jnp.stack(
        [first - coarse_one, second - coarse_two,
         start[2:3 + local] - previous_coarse_two]
    )
    corr = refine(delta)
    fixed_one = values[1] + corr[0]
    fixed_two = values[2] + corr[1]
    head = jnp.where(slot == 0, nodes[0], previous_two + corr[2])
    return (jnp.stack([head, fixed_one, fixed_two])[None], jnp.stack([terms[1], terms[2]])[None])


def solution(mesh):
    return jax.shard_map(
        on_device,
        mesh=mesh,
        in_specs=(P("tm", None, "space", None, None), P("tm", None, "space", None, None)),
        out_specs=(P("tm", None, "space", None, None), P("tm", None, "space", None, None)),
        check_vma=False,
    )
```

```python
import math

import jax
import jax.numpy as jnp
from jax import lax
from jax.sharding import PartitionSpec as P

WEIGHTS = ((5.0 / 24.0, 1.0 / 3.0, -1.0 / 24.0), (-1.0 / 24.0, 1.0 / 3.0, 5.0 / 24.0))
EPS2 = 2.0
HIGHEST = lax.Precision.HIGHEST
TRANSFORM = lax.Precision.HIGH


def react(u):
    return u - u * u * u


def real_basis(size):
    rows = lax.broadcasted_iota(jnp.int32, (size, size), 0)
    cells = lax.broadcasted_iota(jnp.int32, (size, size), 1)
    half = size // 2
    freq = jnp.where(rows <= half, rows, rows - half)
    phase = (freq * cells % size).astype(jnp.float32) * (2.0 * math.pi / size)
    scale = jnp.where((rows == 0) | (rows == half), 1.0 / math.sqrt(size), math.sqrt(2.0 / size))
    return jnp.where(rows <= half, jnp.cos(phase), jnp.sin(phase)) * scale


def wave_square(index, size):
    half = size // 2
    freq = jnp.where(index <= half, index, index - half).astype(jnp.float32)
    kappa = freq * (2.0 * math.pi / size)
    return kappa * kappa


def interp_matrix(size):
    fine_rows = lax.broadcasted_iota(jnp.int32, (2 * size, size), 0)
    coarse_cols = lax.broadcasted_iota(jnp.int32, (2 * size, size), 1)
    base = fine_rows // 2
    odd = fine_rows % 2
    take_base = jnp.where(coarse_cols == base, jnp.where(odd == 0, 1.0, 0.5), 0.0)
    take_next = jnp.where((odd == 1) & (coarse_cols == (base + 1) % size), 0.5, 0.0)
    return (take_base + take_next).astype(jnp.float32)


def spectral_solve(rhs, basis_x, basis_y, basis_z, factor):
    planes, size_y, size_z = rhs.shape
    flat = jnp.dot(rhs.reshape(planes * size_y, size_z), basis_z.T, precision=TRANSFORM)
    field = flat.reshape(planes, size_y, size_z)
    field = jnp.einsum("ky,xyz->kxz", basis_y, field, precision=TRANSFORM)
    field = lax.all_to_all(field, "space", split_axis=0, concat_axis=1, tiled=True)
    field = jnp.einsum("kx,yxz->kyz", basis_x, field, precision=TRANSFORM) * factor
    field = jnp.einsum("kx,kyz->xyz", basis_x, field, precision=TRANSFORM)
    field = lax.all_to_all(field, "space", split_axis=0, concat_axis=1, tiled=True)
    field = jnp.matmul(basis_y.T, field, precision=TRANSFORM)
    flat = jnp.dot(field.reshape(planes * size_y, size_z), basis_z, precision=TRANSFORM)
    return flat.reshape(planes, size_y, size_z)


def pair_average(size):
    rows = lax.broadcasted_iota(jnp.int32, (size, size // 2), 0)
    cols = lax.broadcasted_iota(jnp.int32, (size, size // 2), 1)
    return jnp.where(rows // 2 == cols, 0.5, 0.0).astype(jnp.float32)


def restrict(fields):
    count, planes, size_y, size_z = fields.shape
    pairs = fields.reshape(count, planes // 2, 2, size_y, size_z)
    summed = (pairs[:, :, 0] + pairs[:, :, 1]) * 0.5
    flat = jnp.dot(summed.reshape(-1, size_z), pair_average(size_z), precision=TRANSFORM)
    field = flat.reshape(count, planes // 2, size_y, size_z // 2)
    return jnp.einsum("ya,kpyz->kpaz", pair_average(size_y), field, precision=TRANSFORM)


def fetch(value, offset, back):
    count = lax.axis_size("space")
    if back == 0:
        pairs = [((target + offset) % count, target) for target in range(count)]
        return lax.ppermute(value, "space", pairs)
    slices = lax.axis_size("tm")
    pairs = [
        (((slot - back) % slices) * count + (target + offset) % count, slot * count + target)
        for slot in range(slices)
        for target in range(count)
    ]
    return lax.ppermute(value, ("tm", "space"), pairs)


def cover(low, high, have, local, allowed):
    plan = []
    at = low
    while at < high:
        best = None
        for offset in allowed:
            first = offset * local - have[0]
            last = offset * local + local + have[1]
            if first <= at < last and (best is None or last > best[2]):
                best = (offset, first, last)
        if best is None:
            offset = (at + have[0]) // local
            best = (offset, offset * local - have[0], offset * local + local + have[1])
        upto = min(best[2], high)
        plan.append((best[0], at - best[1], upto - best[1]))
        at = upto
    return plan


def gather_bands(items, back=0):
    local = items[0][0].shape[0] - items[0][1][0] - items[0][1][1]
    allowed = [0] if back == 0 else []
    plans = []
    for band, have, want in items:
        plan = cover(-want[0], local + want[1], have, local, allowed)
        for offset, _, _ in plan:
            if offset not in allowed:
                allowed.append(offset)
        plans.append(plan)
    by_offset = {}
    for i, plan in enumerate(plans):
        for j, (offset, first, last) in enumerate(plan):
            by_offset.setdefault(offset, []).append((i, j, first, last))
    got = {}
    for offset, entries in by_offset.items():
        parts = [items[i][0][first:last] for i, j, first, last in entries]
        if offset == 0 and back == 0:
            for (i, j, first, last), part in zip(entries, parts):
                got[(i, j)] = part
            continue
        moved = fetch(jnp.concatenate(parts, axis=0), offset, back)
        at = 0
        for i, j, first, last in entries:
            got[(i, j)] = moved[at:at + last - first]
            at += last - first
    return [
        jnp.concatenate([got[(i, j)] for j in range(len(plan))], axis=0)
        for i, plan in enumerate(plans)
    ]


def coarse_rate(ext):
    mid = ext[1:-1]
    lap = ext[2:] + ext[:-2]
    lap = lap + jnp.roll(mid, -1, 1) + jnp.roll(mid, 1, 1)
    lap = lap + jnp.roll(mid, -1, 2) + jnp.roll(mid, 1, 2)
    return EPS2 * ((lap - 6.0 * mid) * 0.25) + react(mid)


def spread(values, following, axis):
    middle = 0.5 * (values + following)
    both = jnp.stack([values, middle], axis=axis + 1)
    shape = list(values.shape)
    shape[axis] = shape[axis] * 2
    return both.reshape(shape)


def refine(stacked):
    matrix_y = interp_matrix(stacked.shape[2])
    matrix_z = interp_matrix(stacked.shape[3])
    both = jnp.einsum("kayc,zc->kayz", stacked, matrix_z, precision=TRANSFORM)
    both = jnp.einsum("Yy,kayz->kaYz", matrix_y, both, precision=TRANSFORM)
    planes = stacked.shape[1] - 1
    return spread(both[:, :planes], both[:, 1:], 1)


def coarse_sweep(start, rates, sums):
    first = start[1:-1] + 0.25 * (coarse_rate(start) - rates[0]) + sums[0]
    second = first[1:-1] + 0.25 * (coarse_rate(first) - rates[1]) + sums[1]
    return (first[1:-1], second)


def on_device(fine_nodes, fine_implicit):
    nodes = fine_nodes[0]
    implicit = fine_implicit[0]
    planes, size_y, size_z = (nodes.shape[1], nodes.shape[2], nodes.shape[3])
    devices = lax.axis_size("space")
    size_x = planes * devices
    local_y = size_y // devices
    basis_x = real_basis(size_x)
    basis_y = real_basis(size_y)
    basis_z = real_basis(size_z)
    columns = lax.axis_index("space") * local_y + lax.iota(jnp.int32, local_y)
    lam = wave_square(lax.iota(jnp.int32, size_x), size_x)[:, None, None]
    lam = lam + wave_square(columns, size_y)[None, :, None]
    lam = lam + wave_square(lax.iota(jnp.int32, size_z), size_z)[None, None, :]
    factor = 1.0 / (1.0 + 0.5 * lam)
    explicit_old = react(nodes)
    rates_old = explicit_old + implicit
    values = [nodes[0]]
    terms = [implicit[0]]
    for m in range(2):
        w = WEIGHTS[m]
        quad = 0.5 * (w[0] * rates_old[0] + w[1] * rates_old[1] + w[2] * rates_old[2])
        rhs = (
            values[m] + 0.25 * (react(values[m]) - explicit_old[m]) - 0.25 * implicit[m + 1] + quad
        )
        solved = spectral_solve(rhs, basis_x, basis_y, basis_z, factor)
        values.append(solved)
        terms.append((solved - rhs) * 4.0)
    fresh = jnp.stack(values)
    rates_new = react(fresh) + jnp.stack(terms)
    sums = [0.5 * (w[0] * rates_new[0] + w[1] * rates_new[1] + w[2] * rates_new[2]) for w in WEIGHTS]
    coarse = restrict(jnp.stack([values[0], values[1], values[2], sums[0], sums[1]]))
    slot = lax.axis_index("tm")
    slices = lax.axis_size("tm")
    local = planes // 2
    wide = gather_bands(
        [(coarse[0], (0, 0), (2, 3)), (coarse[1], (0, 0), (1, 2)), (coarse[3], (0, 0), (1, 2)),
         (coarse[4], (0, 0), (0, 1)), (coarse[2], (0, 0), (0, 1))]
    )
    previous_two = fetch(values[2], 0, 1)
    previous_two, wide = lax.optimization_barrier((previous_two, wide))
    start_c = wide[0]
    rates_c = (coarse_rate(start_c), coarse_rate(wide[1]))
    sums_c = (wide[2], wide[3])
    coarse_one = wide[1][1:2 + local]
    coarse_two = wide[4]
    start = start_c
    previous_coarse_two = None
    for section in range(slices - 1):
        first, second = coarse_sweep(start, rates_c, sums_c)
        items = [(second, (0, 1), (2, 3))]
        if previous_coarse_two is None:
            items.append((coarse_two, (0, 1), (0, 1)))
        received = gather_bands(items, back=1)
        if previous_coarse_two is None:
            previous_coarse_two = received[1]
        start = jnp.where(slot == 0, start_c, received[0])
    first, second = coarse_sweep(start, rates_c, sums_c)
    delta = jnp.stack(
        [first - coarse_one, second - coarse_two,
         start[2:3 + local] - previous_coarse_two]
    )
    corr = refine(delta)
    fixed_one = values[1] + corr[0]
    fixed_two = values[2] + corr[1]
    head = jnp.where(slot == 0, nodes[0], previous_two + corr[2])
    return (jnp.stack([head, fixed_one, fixed_two])[None], jnp.stack([terms[1], terms[2]])[None])


def solution(mesh):
    return jax.shard_map(
        on_device,
        mesh=mesh,
        in_specs=(P("tm", None, "space", None, None), P("tm", None, "space", None, None)),
        out_specs=(P("tm", None, "space", None, None), P("tm", None, "space", None, None)),
        check_vma=False,
    )
```

```python
import math

import jax
import jax.numpy as jnp
from jax import lax
from jax.sharding import PartitionSpec as P

WEIGHTS = ((5.0 / 24.0, 1.0 / 3.0, -1.0 / 24.0), (-1.0 / 24.0, 1.0 / 3.0, 5.0 / 24.0))
EPS2 = 2.0
HIGHEST = lax.Precision.HIGHEST
TRANSFORM = lax.Precision.HIGH


def react(u):
    return u - u * u * u


def real_basis(size):
    rows = lax.broadcasted_iota(jnp.int32, (size, size), 0)
    cells = lax.broadcasted_iota(jnp.int32, (size, size), 1)
    half = size // 2
    freq = jnp.where(rows <= half, rows, rows - half)
    phase = (freq * cells % size).astype(jnp.float32) * (2.0 * math.pi / size)
    scale = jnp.where((rows == 0) | (rows == half), 1.0 / math.sqrt(size), math.sqrt(2.0 / size))
    return jnp.where(rows <= half, jnp.cos(phase), jnp.sin(phase)) * scale


def wave_square(index, size):
    half = size // 2
    freq = jnp.where(index <= half, index, index - half).astype(jnp.float32)
    kappa = freq * (2.0 * math.pi / size)
    return kappa * kappa


def interp_matrix(size):
    fine_rows = lax.broadcasted_iota(jnp.int32, (2 * size, size), 0)
    coarse_cols = lax.broadcasted_iota(jnp.int32, (2 * size, size), 1)
    base = fine_rows // 2
    odd = fine_rows % 2
    take_base = jnp.where(coarse_cols == base, jnp.where(odd == 0, 1.0, 0.5), 0.0)
    take_next = jnp.where((odd == 1) & (coarse_cols == (base + 1) % size), 0.5, 0.0)
    return (take_base + take_next).astype(jnp.float32)


def spectral_solve(rhs, basis_x, basis_y, basis_z, factor):
    planes, size_y, size_z = rhs.shape
    flat = jnp.dot(rhs.reshape(planes * size_y, size_z), basis_z.T, precision=TRANSFORM)
    field = flat.reshape(planes, size_y, size_z)
    field = jnp.einsum("ky,xyz->kxz", basis_y, field, precision=TRANSFORM)
    field = lax.all_to_all(field, "space", split_axis=0, concat_axis=1, tiled=True)
    field = jnp.einsum("kx,yxz->kyz", basis_x, field, precision=TRANSFORM) * factor
    field = jnp.einsum("kx,kyz->xyz", basis_x, field, precision=TRANSFORM)
    field = lax.all_to_all(field, "space", split_axis=0, concat_axis=1, tiled=True)
    field = jnp.matmul(basis_y.T, field, precision=TRANSFORM)
    flat = jnp.dot(field.reshape(planes * size_y, size_z), basis_z, precision=TRANSFORM)
    return flat.reshape(planes, size_y, size_z)


def pair_average(size):
    rows = lax.broadcasted_iota(jnp.int32, (size, size // 2), 0)
    cols = lax.broadcasted_iota(jnp.int32, (size, size // 2), 1)
    return jnp.where(rows // 2 == cols, 0.5, 0.0).astype(jnp.float32)


def restrict(fields):
    count, planes, size_y, size_z = fields.shape
    pairs = fields.reshape(count, planes // 2, 2, size_y, size_z)
    summed = (pairs[:, :, 0] + pairs[:, :, 1]) * 0.5
    flat = jnp.dot(summed.reshape(-1, size_z), pair_average(size_z), precision=TRANSFORM)
    field = flat.reshape(count, planes // 2, size_y, size_z // 2)
    return jnp.einsum("ya,kpyz->kpaz", pair_average(size_y), field, precision=TRANSFORM)


def fetch(value, offset, back):
    count = lax.axis_size("space")
    if back == 0:
        pairs = [((target + offset) % count, target) for target in range(count)]
        return lax.ppermute(value, "space", pairs)
    slices = lax.axis_size("tm")
    pairs = [
        (((slot - back) % slices) * count + (target + offset) % count, slot * count + target)
        for slot in range(slices)
        for target in range(count)
    ]
    return lax.ppermute(value, ("tm", "space"), pairs)


def cover(low, high, have, local, allowed):
    plan = []
    at = low
    while at < high:
        best = None
        for offset in allowed:
            first = offset * local - have[0]
            last = offset * local + local + have[1]
            if first <= at < last and (best is None or last > best[2]):
                best = (offset, first, last)
        if best is None:
            offset = (at + have[0]) // local
            best = (offset, offset * local - have[0], offset * local + local + have[1])
        upto = min(best[2], high)
        plan.append((best[0], at - best[1], upto - best[1]))
        at = upto
    return plan


def gather_bands(items, back=0):
    local = items[0][0].shape[0] - items[0][1][0] - items[0][1][1]
    allowed = [0] if back == 0 else []
    plans = []
    for band, have, want in items:
        plan = cover(-want[0], local + want[1], have, local, allowed)
        for offset, _, _ in plan:
            if offset not in allowed:
                allowed.append(offset)
        plans.append(plan)
    by_offset = {}
    for i, plan in enumerate(plans):
        for j, (offset, first, last) in enumerate(plan):
            by_offset.setdefault(offset, []).append((i, j, first, last))
    got = {}
    for offset, entries in by_offset.items():
        parts = [items[i][0][first:last] for i, j, first, last in entries]
        if offset == 0 and back == 0:
            for (i, j, first, last), part in zip(entries, parts):
                got[(i, j)] = part
            continue
        moved = fetch(jnp.concatenate(parts, axis=0), offset, back)
        at = 0
        for i, j, first, last in entries:
            got[(i, j)] = moved[at:at + last - first]
            at += last - first
    return [
        jnp.concatenate([got[(i, j)] for j in range(len(plan))], axis=0)
        for i, plan in enumerate(plans)
    ]


def coarse_rate(ext):
    mid = ext[1:-1]
    lap = ext[2:] + ext[:-2]
    lap = lap + jnp.roll(mid, -1, 1) + jnp.roll(mid, 1, 1)
    lap = lap + jnp.roll(mid, -1, 2) + jnp.roll(mid, 1, 2)
    return EPS2 * ((lap - 6.0 * mid) * 0.25) + react(mid)


def spread(values, following, axis):
    middle = 0.5 * (values + following)
    both = jnp.stack([values, middle], axis=axis + 1)
    shape = list(values.shape)
    shape[axis] = shape[axis] * 2
    return both.reshape(shape)


def refine(stacked):
    matrix_y = interp_matrix(stacked.shape[2])
    matrix_z = interp_matrix(stacked.shape[3])
    both = jnp.einsum("kayc,zc->kayz", stacked, matrix_z, precision=TRANSFORM)
    both = jnp.einsum("Yy,kayz->kaYz", matrix_y, both, precision=TRANSFORM)
    planes = stacked.shape[1] - 1
    return spread(both[:, :planes], both[:, 1:], 1)


def coarse_sweep(start, rates, sums):
    first = start[1:-1] + 0.25 * (coarse_rate(start) - rates[0]) + sums[0]
    second = first[1:-1] + 0.25 * (coarse_rate(first) - rates[1]) + sums[1]
    return (first[1:-1], second)


def on_device(fine_nodes, fine_implicit):
    nodes = fine_nodes[0]
    implicit = fine_implicit[0]
    planes, size_y, size_z = (nodes.shape[1], nodes.shape[2], nodes.shape[3])
    devices = lax.axis_size("space")
    size_x = planes * devices
    local_y = size_y // devices
    basis_x = real_basis(size_x)
    basis_y = real_basis(size_y)
    basis_z = real_basis(size_z)
    columns = lax.axis_index("space") * local_y + lax.iota(jnp.int32, local_y)
    lam = wave_square(lax.iota(jnp.int32, size_x), size_x)[:, None, None]
    lam = lam + wave_square(columns, size_y)[None, :, None]
    lam = lam + wave_square(lax.iota(jnp.int32, size_z), size_z)[None, None, :]
    factor = 1.0 / (1.0 + 0.5 * lam)
    explicit_old = react(nodes)
    rates_old = explicit_old + implicit
    values = [nodes[0]]
    terms = [implicit[0]]
    for m in range(2):
        w = WEIGHTS[m]
        quad = 0.5 * (w[0] * rates_old[0] + w[1] * rates_old[1] + w[2] * rates_old[2])
        rhs = (
            values[m] + 0.25 * (react(values[m]) - explicit_old[m]) - 0.25 * implicit[m + 1] + quad
        )
        solved = spectral_solve(rhs, basis_x, basis_y, basis_z, factor)
        values.append(solved)
        terms.append((solved - rhs) * 4.0)
    fresh = jnp.stack(values)
    rates_new = react(fresh) + jnp.stack(terms)
    sums = [0.5 * (w[0] * rates_new[0] + w[1] * rates_new[1] + w[2] * rates_new[2]) for w in WEIGHTS]
    coarse = restrict(jnp.stack([values[0], values[1], values[2], sums[0], sums[1]]))
    slot = lax.axis_index("tm")
    slices = lax.axis_size("tm")
    local = planes // 2
    wide = gather_bands(
        [(coarse[0], (0, 0), (2, 3)), (coarse[1], (0, 0), (1, 2)), (coarse[3], (0, 0), (1, 2)),
         (coarse[4], (0, 0), (0, 1)), (coarse[2], (0, 0), (0, 1))]
    )
    start_c = wide[0]
    rates_c = (coarse_rate(start_c), coarse_rate(wide[1]))
    sums_c = (wide[2], wide[3])
    coarse_one = wide[1][1:2 + local]
    coarse_two = wide[4]
    start = start_c
    previous_coarse_two = None
    for section in range(slices - 1):
        first, second = coarse_sweep(start, rates_c, sums_c)
        items = [(second, (0, 1), (2, 3))]
        if previous_coarse_two is None:
            items.append((coarse_two, (0, 1), (0, 1)))
        received = gather_bands(items, back=1)
        if previous_coarse_two is None:
            previous_two = fetch(values[2], 0, 1)
            previous_two, received = lax.optimization_barrier((previous_two, received))
            previous_coarse_two = received[1]
        start = jnp.where(slot == 0, start_c, received[0])
    first, second = coarse_sweep(start, rates_c, sums_c)
    delta = jnp.stack(
        [first - coarse_one, second - coarse_two,
         start[2:3 + local] - previous_coarse_two]
    )
    corr = refine(delta)
    fixed_one = values[1] + corr[0]
    fixed_two = values[2] + corr[1]
    head = jnp.where(slot == 0, nodes[0], previous_two + corr[2])
    return (jnp.stack([head, fixed_one, fixed_two])[None], jnp.stack([terms[1], terms[2]])[None])


def solution(mesh):
    return jax.shard_map(
        on_device,
        mesh=mesh,
        in_specs=(P("tm", None, "space", None, None), P("tm", None, "space", None, None)),
        out_specs=(P("tm", None, "space", None, None), P("tm", None, "space", None, None)),
        check_vma=False,
    )
```

```python
import math

import jax
import jax.numpy as jnp
from jax import lax
from jax.sharding import PartitionSpec as P

WEIGHTS = ((5.0 / 24.0, 1.0 / 3.0, -1.0 / 24.0), (-1.0 / 24.0, 1.0 / 3.0, 5.0 / 24.0))
EPS2 = 2.0
HIGHEST = lax.Precision.HIGHEST
TRANSFORM = lax.Precision.HIGH


def react(u):
    return u - u * u * u


def real_basis(size):
    rows = lax.broadcasted_iota(jnp.int32, (size, size), 0)
    cells = lax.broadcasted_iota(jnp.int32, (size, size), 1)
    half = size // 2
    freq = jnp.where(rows <= half, rows, rows - half)
    phase = (freq * cells % size).astype(jnp.float32) * (2.0 * math.pi / size)
    scale = jnp.where((rows == 0) | (rows == half), 1.0 / math.sqrt(size), math.sqrt(2.0 / size))
    return jnp.where(rows <= half, jnp.cos(phase), jnp.sin(phase)) * scale


def wave_square(index, size):
    half = size // 2
    freq = jnp.where(index <= half, index, index - half).astype(jnp.float32)
    kappa = freq * (2.0 * math.pi / size)
    return kappa * kappa


def interp_matrix(size):
    fine_rows = lax.broadcasted_iota(jnp.int32, (2 * size, size), 0)
    coarse_cols = lax.broadcasted_iota(jnp.int32, (2 * size, size), 1)
    base = fine_rows // 2
    odd = fine_rows % 2
    take_base = jnp.where(coarse_cols == base, jnp.where(odd == 0, 1.0, 0.5), 0.0)
    take_next = jnp.where((odd == 1) & (coarse_cols == (base + 1) % size), 0.5, 0.0)
    return (take_base + take_next).astype(jnp.float32)


def spectral_solve(rhs, basis_x, basis_y, basis_z, factor):
    planes, size_y, size_z = rhs.shape
    flat = jnp.dot(rhs.reshape(planes * size_y, size_z), basis_z.T, precision=TRANSFORM)
    field = flat.reshape(planes, size_y, size_z)
    field = jnp.einsum("ky,xyz->kxz", basis_y, field, precision=TRANSFORM)
    field = lax.all_to_all(field, "space", split_axis=0, concat_axis=1, tiled=True)
    field = jnp.einsum("kx,yxz->kyz", basis_x, field, precision=TRANSFORM) * factor
    field = jnp.einsum("kx,kyz->xyz", basis_x, field, precision=TRANSFORM)
    field = lax.all_to_all(field, "space", split_axis=0, concat_axis=1, tiled=True)
    field = jnp.matmul(basis_y.T, field, precision=TRANSFORM)
    flat = jnp.dot(field.reshape(planes * size_y, size_z), basis_z, precision=TRANSFORM)
    return flat.reshape(planes, size_y, size_z)


def pair_average(size):
    rows = lax.broadcasted_iota(jnp.int32, (size, size // 2), 0)
    cols = lax.broadcasted_iota(jnp.int32, (size, size // 2), 1)
    return jnp.where(rows // 2 == cols, 0.5, 0.0).astype(jnp.float32)


def restrict(fields):
    count, planes, size_y, size_z = fields.shape
    pairs = fields.reshape(count, planes // 2, 2, size_y, size_z)
    summed = (pairs[:, :, 0] + pairs[:, :, 1]) * 0.5
    flat = jnp.dot(summed.reshape(-1, size_z), pair_average(size_z), precision=TRANSFORM)
    field = flat.reshape(count, planes // 2, size_y, size_z // 2)
    return jnp.einsum("ya,kpyz->kpaz", pair_average(size_y), field, precision=TRANSFORM)


def fetch(value, offset, back):
    count = lax.axis_size("space")
    if back == 0:
        pairs = [((target + offset) % count, target) for target in range(count)]
        return lax.ppermute(value, "space", pairs)
    slices = lax.axis_size("tm")
    pairs = [
        (((slot - back) % slices) * count + (target + offset) % count, slot * count + target)
        for slot in range(slices)
        for target in range(count)
    ]
    return lax.ppermute(value, ("tm", "space"), pairs)


def cover(low, high, have, local, allowed):
    plan = []
    at = low
    while at < high:
        best = None
        for offset in allowed:
            first = offset * local - have[0]
            last = offset * local + local + have[1]
            if first <= at < last and (best is None or last > best[2]):
                best = (offset, first, last)
        if best is None:
            offset = (at + have[0]) // local
            best = (offset, offset * local - have[0], offset * local + local + have[1])
        upto = min(best[2], high)
        plan.append((best[0], at - best[1], upto - best[1]))
        at = upto
    return plan


def gather_bands(items, back=0):
    local = items[0][0].shape[0] - items[0][1][0] - items[0][1][1]
    allowed = [0] if back == 0 else []
    plans = []
    for band, have, want in items:
        plan = cover(-want[0], local + want[1], have, local, allowed)
        for offset, _, _ in plan:
            if offset not in allowed:
                allowed.append(offset)
        plans.append(plan)
    by_offset = {}
    for i, plan in enumerate(plans):
        for j, (offset, first, last) in enumerate(plan):
            by_offset.setdefault(offset, []).append((i, j, first, last))
    got = {}
    for offset, entries in by_offset.items():
        parts = [items[i][0][first:last] for i, j, first, last in entries]
        if offset == 0 and back == 0:
            for (i, j, first, last), part in zip(entries, parts):
                got[(i, j)] = part
            continue
        moved = fetch(jnp.concatenate(parts, axis=0), offset, back)
        at = 0
        for i, j, first, last in entries:
            got[(i, j)] = moved[at:at + last - first]
            at += last - first
    return [
        jnp.concatenate([got[(i, j)] for j in range(len(plan))], axis=0)
        for i, plan in enumerate(plans)
    ]


def coarse_rate(ext):
    mid = ext[1:-1]
    lap = ext[2:] + ext[:-2]
    lap = lap + jnp.roll(mid, -1, 1) + jnp.roll(mid, 1, 1)
    lap = lap + jnp.roll(mid, -1, 2) + jnp.roll(mid, 1, 2)
    return EPS2 * ((lap - 6.0 * mid) * 0.25) + react(mid)


def spread(values, following, axis):
    middle = 0.5 * (values + following)
    both = jnp.stack([values, middle], axis=axis + 1)
    shape = list(values.shape)
    shape[axis] = shape[axis] * 2
    return both.reshape(shape)


def refine(stacked):
    matrix_y = interp_matrix(stacked.shape[2])
    matrix_z = interp_matrix(stacked.shape[3])
    both = jnp.einsum("kayc,zc->kayz", stacked, matrix_z, precision=TRANSFORM)
    both = jnp.einsum("Yy,kayz->kaYz", matrix_y, both, precision=TRANSFORM)
    planes = stacked.shape[1] - 1
    return spread(both[:, :planes], both[:, 1:], 1)


def coarse_sweep(start, rates, sums):
    first = start[1:-1] + 0.25 * (coarse_rate(start) - rates[0]) + sums[0]
    second = first[1:-1] + 0.25 * (coarse_rate(first) - rates[1]) + sums[1]
    return (first[1:-1], second)


def on_device(fine_nodes, fine_implicit):
    nodes = fine_nodes[0]
    implicit = fine_implicit[0]
    planes, size_y, size_z = (nodes.shape[1], nodes.shape[2], nodes.shape[3])
    devices = lax.axis_size("space")
    size_x = planes * devices
    local_y = size_y // devices
    basis_x = real_basis(size_x)
    basis_y = real_basis(size_y)
    basis_z = real_basis(size_z)
    columns = lax.axis_index("space") * local_y + lax.iota(jnp.int32, local_y)
    lam = wave_square(lax.iota(jnp.int32, size_x), size_x)[:, None, None]
    lam = lam + wave_square(columns, size_y)[None, :, None]
    lam = lam + wave_square(lax.iota(jnp.int32, size_z), size_z)[None, None, :]
    factor = 1.0 / (1.0 + 0.5 * lam)
    explicit_old = react(nodes)
    rates_old = explicit_old + implicit
    values = [nodes[0]]
    terms = [implicit[0]]
    for m in range(2):
        w = WEIGHTS[m]
        quad = 0.5 * (w[0] * rates_old[0] + w[1] * rates_old[1] + w[2] * rates_old[2])
        rhs = (
            values[m] + 0.25 * (react(values[m]) - explicit_old[m]) - 0.25 * implicit[m + 1] + quad
        )
        solved = spectral_solve(rhs, basis_x, basis_y, basis_z, factor)
        values.append(solved)
        terms.append((solved - rhs) * 4.0)
    fresh = jnp.stack(values)
    rates_new = react(fresh) + jnp.stack(terms)
    sums = [0.5 * (w[0] * rates_new[0] + w[1] * rates_new[1] + w[2] * rates_new[2]) for w in WEIGHTS]
    coarse = restrict(jnp.stack([values[0], values[1], values[2], sums[0], sums[1]]))
    slot = lax.axis_index("tm")
    slices = lax.axis_size("tm")
    local = planes // 2
    wide = gather_bands(
        [(coarse[0], (0, 0), (2, 3)), (coarse[1], (0, 0), (1, 2)), (coarse[3], (0, 0), (1, 2)),
         (coarse[4], (0, 0), (0, 1)), (coarse[2], (0, 0), (0, 1))]
    )
    start_c = wide[0]
    rates_c = (coarse_rate(start_c), coarse_rate(wide[1]))
    sums_c = (wide[2], wide[3])
    coarse_one = wide[1][1:2 + local]
    coarse_two = wide[4]
    start = start_c
    previous_coarse_two = None
    for section in range(slices - 1):
        first, second = coarse_sweep(start, rates_c, sums_c)
        items = [(second, (0, 1), (2, 3))]
        if previous_coarse_two is None:
            items.append((coarse_two, (0, 1), (0, 1)))
        received = gather_bands(items, back=1)
        if previous_coarse_two is None:
            previous_coarse_two = received[1]
        if section == slices - 2:
            previous_two = fetch(values[2], 0, 1)
            previous_two, received = lax.optimization_barrier((previous_two, received))
        start = jnp.where(slot == 0, start_c, received[0])
    first, second = coarse_sweep(start, rates_c, sums_c)
    delta = jnp.stack(
        [first - coarse_one, second - coarse_two,
         start[2:3 + local] - previous_coarse_two]
    )
    corr = refine(delta)
    fixed_one = values[1] + corr[0]
    fixed_two = values[2] + corr[1]
    head = jnp.where(slot == 0, nodes[0], previous_two + corr[2])
    return (jnp.stack([head, fixed_one, fixed_two])[None], jnp.stack([terms[1], terms[2]])[None])


def solution(mesh):
    return jax.shard_map(
        on_device,
        mesh=mesh,
        in_specs=(P("tm", None, "space", None, None), P("tm", None, "space", None, None)),
        out_specs=(P("tm", None, "space", None, None), P("tm", None, "space", None, None)),
        check_vma=False,
    )
```

```python
import math

import jax
import jax.numpy as jnp
from jax import lax
from jax.sharding import PartitionSpec as P

WEIGHTS = ((5.0 / 24.0, 1.0 / 3.0, -1.0 / 24.0), (-1.0 / 24.0, 1.0 / 3.0, 5.0 / 24.0))
EPS2 = 2.0
HIGHEST = lax.Precision.HIGHEST
TRANSFORM = lax.Precision.HIGH


def react(u):
    return u - u * u * u


def real_basis(size):
    rows = lax.broadcasted_iota(jnp.int32, (size, size), 0)
    cells = lax.broadcasted_iota(jnp.int32, (size, size), 1)
    half = size // 2
    freq = jnp.where(rows <= half, rows, rows - half)
    phase = (freq * cells % size).astype(jnp.float32) * (2.0 * math.pi / size)
    scale = jnp.where((rows == 0) | (rows == half), 1.0 / math.sqrt(size), math.sqrt(2.0 / size))
    return jnp.where(rows <= half, jnp.cos(phase), jnp.sin(phase)) * scale


def wave_square(index, size):
    half = size // 2
    freq = jnp.where(index <= half, index, index - half).astype(jnp.float32)
    kappa = freq * (2.0 * math.pi / size)
    return kappa * kappa


def interp_matrix(size):
    fine_rows = lax.broadcasted_iota(jnp.int32, (2 * size, size), 0)
    coarse_cols = lax.broadcasted_iota(jnp.int32, (2 * size, size), 1)
    base = fine_rows // 2
    odd = fine_rows % 2
    take_base = jnp.where(coarse_cols == base, jnp.where(odd == 0, 1.0, 0.5), 0.0)
    take_next = jnp.where((odd == 1) & (coarse_cols == (base + 1) % size), 0.5, 0.0)
    return (take_base + take_next).astype(jnp.float32)


def spectral_solve(rhs, basis_x, basis_y, basis_z, factor):
    planes, size_y, size_z = rhs.shape
    flat = jnp.dot(rhs.reshape(planes * size_y, size_z), basis_z.T, precision=TRANSFORM)
    field = flat.reshape(planes, size_y, size_z)
    field = jnp.einsum("ky,xyz->kxz", basis_y, field, precision=TRANSFORM)
    field = lax.all_to_all(field, "space", split_axis=0, concat_axis=1, tiled=True)
    field = jnp.einsum("kx,yxz->kyz", basis_x, field, precision=TRANSFORM) * factor
    field = jnp.einsum("kx,kyz->xyz", basis_x, field, precision=TRANSFORM)
    field = lax.all_to_all(field, "space", split_axis=0, concat_axis=1, tiled=True)
    field = jnp.matmul(basis_y.T, field, precision=TRANSFORM)
    flat = jnp.dot(field.reshape(planes * size_y, size_z), basis_z, precision=TRANSFORM)
    return flat.reshape(planes, size_y, size_z)


def pair_average(size):
    rows = lax.broadcasted_iota(jnp.int32, (size, size // 2), 0)
    cols = lax.broadcasted_iota(jnp.int32, (size, size // 2), 1)
    return jnp.where(rows // 2 == cols, 0.5, 0.0).astype(jnp.float32)


def restrict(fields):
    count, planes, size_y, size_z = fields.shape
    pairs = fields.reshape(count, planes // 2, 2, size_y, size_z)
    summed = (pairs[:, :, 0] + pairs[:, :, 1]) * 0.5
    flat = jnp.dot(summed.reshape(-1, size_z), pair_average(size_z), precision=TRANSFORM)
    field = flat.reshape(count, planes // 2, size_y, size_z // 2)
    return jnp.einsum("ya,kpyz->kpaz", pair_average(size_y), field, precision=TRANSFORM)


def fetch(value, offset, back):
    count = lax.axis_size("space")
    if back == 0:
        pairs = [((target + offset) % count, target) for target in range(count)]
        return lax.ppermute(value, "space", pairs)
    slices = lax.axis_size("tm")
    pairs = [
        (((slot - back) % slices) * count + (target + offset) % count, slot * count + target)
        for slot in range(slices)
        for target in range(count)
    ]
    return lax.ppermute(value, ("tm", "space"), pairs)


def cover(low, high, have, local, allowed):
    plan = []
    at = low
    while at < high:
        best = None
        for offset in allowed:
            first = offset * local - have[0]
            last = offset * local + local + have[1]
            if first <= at < last and (best is None or last > best[2]):
                best = (offset, first, last)
        if best is None:
            offset = (at + have[0]) // local
            best = (offset, offset * local - have[0], offset * local + local + have[1])
        upto = min(best[2], high)
        plan.append((best[0], at - best[1], upto - best[1]))
        at = upto
    return plan


def gather_bands(items, back=0):
    local = items[0][0].shape[0] - items[0][1][0] - items[0][1][1]
    allowed = [0] if back == 0 else []
    plans = []
    for band, have, want in items:
        plan = cover(-want[0], local + want[1], have, local, allowed)
        for offset, _, _ in plan:
            if offset not in allowed:
                allowed.append(offset)
        plans.append(plan)
    by_offset = {}
    for i, plan in enumerate(plans):
        for j, (offset, first, last) in enumerate(plan):
            by_offset.setdefault(offset, []).append((i, j, first, last))
    got = {}
    for offset, entries in by_offset.items():
        parts = [items[i][0][first:last] for i, j, first, last in entries]
        if offset == 0 and back == 0:
            for (i, j, first, last), part in zip(entries, parts):
                got[(i, j)] = part
            continue
        moved = fetch(jnp.concatenate(parts, axis=0), offset, back)
        at = 0
        for i, j, first, last in entries:
            got[(i, j)] = moved[at:at + last - first]
            at += last - first
    return [
        jnp.concatenate([got[(i, j)] for j in range(len(plan))], axis=0)
        for i, plan in enumerate(plans)
    ]


def coarse_rate(ext):
    mid = ext[1:-1]
    lap = ext[2:] + ext[:-2]
    lap = lap + jnp.roll(mid, -1, 1) + jnp.roll(mid, 1, 1)
    lap = lap + jnp.roll(mid, -1, 2) + jnp.roll(mid, 1, 2)
    return EPS2 * ((lap - 6.0 * mid) * 0.25) + react(mid)


def spread(values, following, axis):
    middle = 0.5 * (values + following)
    both = jnp.stack([values, middle], axis=axis + 1)
    shape = list(values.shape)
    shape[axis] = shape[axis] * 2
    return both.reshape(shape)


def refine(stacked):
    matrix_y = interp_matrix(stacked.shape[2])
    matrix_z = interp_matrix(stacked.shape[3])
    both = jnp.einsum("kayc,zc->kayz", stacked, matrix_z, precision=TRANSFORM)
    both = jnp.einsum("Yy,kayz->kaYz", matrix_y, both, precision=TRANSFORM)
    planes = stacked.shape[1] - 1
    return spread(both[:, :planes], both[:, 1:], 1)


def coarse_sweep(start, rates, sums):
    first = start[1:-1] + 0.25 * (coarse_rate(start) - rates[0]) + sums[0]
    second = first[1:-1] + 0.25 * (coarse_rate(first) - rates[1]) + sums[1]
    return (first[1:-1], second)


def on_device(fine_nodes, fine_implicit):
    nodes = fine_nodes[0]
    implicit = fine_implicit[0]
    planes, size_y, size_z = (nodes.shape[1], nodes.shape[2], nodes.shape[3])
    devices = lax.axis_size("space")
    size_x = planes * devices
    local_y = size_y // devices
    basis_x = real_basis(size_x)
    basis_y = real_basis(size_y)
    basis_z = real_basis(size_z)
    columns = lax.axis_index("space") * local_y + lax.iota(jnp.int32, local_y)
    lam = wave_square(lax.iota(jnp.int32, size_x), size_x)[:, None, None]
    lam = lam + wave_square(columns, size_y)[None, :, None]
    lam = lam + wave_square(lax.iota(jnp.int32, size_z), size_z)[None, None, :]
    factor = 1.0 / (1.0 + 0.5 * lam)
    explicit_old = react(nodes)
    rates_old = explicit_old + implicit
    values = [nodes[0]]
    terms = [implicit[0]]
    for m in range(2):
        w = WEIGHTS[m]
        quad = 0.5 * (w[0] * rates_old[0] + w[1] * rates_old[1] + w[2] * rates_old[2])
        rhs = (
            values[m] + 0.25 * (react(values[m]) - explicit_old[m]) - 0.25 * implicit[m + 1] + quad
        )
        solved = spectral_solve(rhs, basis_x, basis_y, basis_z, factor)
        values.append(solved)
        terms.append((solved - rhs) * 4.0)
    fresh = jnp.stack(values)
    rates_new = react(fresh) + jnp.stack(terms)
    sums = [0.5 * (w[0] * rates_new[0] + w[1] * rates_new[1] + w[2] * rates_new[2]) for w in WEIGHTS]
    coarse = restrict(jnp.stack([values[0], values[1], values[2], sums[0], sums[1]]))
    slot = lax.axis_index("tm")
    slices = lax.axis_size("tm")
    local = planes // 2
    wide = gather_bands(
        [(coarse[0], (0, 0), (2, 3)), (coarse[1], (0, 0), (1, 2)), (coarse[3], (0, 0), (1, 2)),
         (coarse[4], (0, 0), (0, 1)), (coarse[2], (0, 0), (0, 1))]
    )
    start_c = wide[0]
    rates_c = (coarse_rate(start_c), coarse_rate(wide[1]))
    sums_c = (wide[2], wide[3])
    coarse_one = wide[1][1:2 + local]
    coarse_two = wide[4]
    start = start_c
    previous_coarse_two = None
    for section in range(slices - 1):
        first, second = coarse_sweep(start, rates_c, sums_c)
        items = [(second, (0, 1), (2, 3))]
        if section == slices - 2:
            items.append((coarse_two, (0, 1), (0, 1)))
        received = gather_bands(items, back=1)
        if section == slices - 2:
            previous_coarse_two = received[1]
        if section == slices - 2:
            previous_two = fetch(values[2], 0, 1)
            previous_two, received = lax.optimization_barrier((previous_two, received))
        start = jnp.where(slot == 0, start_c, received[0])
    first, second = coarse_sweep(start, rates_c, sums_c)
    delta = jnp.stack(
        [first - coarse_one, second - coarse_two,
         start[2:3 + local] - previous_coarse_two]
    )
    corr = refine(delta)
    fixed_one = values[1] + corr[0]
    fixed_two = values[2] + corr[1]
    head = jnp.where(slot == 0, nodes[0], previous_two + corr[2])
    return (jnp.stack([head, fixed_one, fixed_two])[None], jnp.stack([terms[1], terms[2]])[None])


def solution(mesh):
    return jax.shard_map(
        on_device,
        mesh=mesh,
        in_specs=(P("tm", None, "space", None, None), P("tm", None, "space", None, None)),
        out_specs=(P("tm", None, "space", None, None), P("tm", None, "space", None, None)),
        check_vma=False,
    )
```

```python
import math

import jax
import jax.numpy as jnp
from jax import lax
from jax.sharding import PartitionSpec as P

WEIGHTS = ((5.0 / 24.0, 1.0 / 3.0, -1.0 / 24.0), (-1.0 / 24.0, 1.0 / 3.0, 5.0 / 24.0))
EPS2 = 2.0
HIGHEST = lax.Precision.HIGHEST
TRANSFORM = lax.Precision.HIGH


def react(u):
    return u - u * u * u


def real_basis(size):
    rows = lax.broadcasted_iota(jnp.int32, (size, size), 0)
    cells = lax.broadcasted_iota(jnp.int32, (size, size), 1)
    half = size // 2
    freq = jnp.where(rows <= half, rows, rows - half)
    phase = (freq * cells % size).astype(jnp.float32) * (2.0 * math.pi / size)
    scale = jnp.where((rows == 0) | (rows == half), 1.0 / math.sqrt(size), math.sqrt(2.0 / size))
    return jnp.where(rows <= half, jnp.cos(phase), jnp.sin(phase)) * scale


def wave_square(index, size):
    half = size // 2
    freq = jnp.where(index <= half, index, index - half).astype(jnp.float32)
    kappa = freq * (2.0 * math.pi / size)
    return kappa * kappa


def interp_matrix(size):
    fine_rows = lax.broadcasted_iota(jnp.int32, (2 * size, size), 0)
    coarse_cols = lax.broadcasted_iota(jnp.int32, (2 * size, size), 1)
    base = fine_rows // 2
    odd = fine_rows % 2
    take_base = jnp.where(coarse_cols == base, jnp.where(odd == 0, 1.0, 0.5), 0.0)
    take_next = jnp.where((odd == 1) & (coarse_cols == (base + 1) % size), 0.5, 0.0)
    return (take_base + take_next).astype(jnp.float32)


def spectral_solve(rhs, basis_x, basis_y, basis_z, factor):
    planes, size_y, size_z = rhs.shape
    flat = jnp.dot(rhs.reshape(planes * size_y, size_z), basis_z.T, precision=TRANSFORM)
    field = flat.reshape(planes, size_y, size_z)
    field = jnp.einsum("ky,xyz->kxz", basis_y, field, precision=TRANSFORM)
    field = lax.all_to_all(field, "space", split_axis=0, concat_axis=1, tiled=True)
    field = jnp.einsum("kx,yxz->kyz", basis_x, field, precision=TRANSFORM) * factor
    field = jnp.einsum("kx,kyz->xyz", basis_x, field, precision=TRANSFORM)
    field = lax.all_to_all(field, "space", split_axis=0, concat_axis=1, tiled=True)
    field = jnp.matmul(basis_y.T, field, precision=TRANSFORM)
    flat = jnp.dot(field.reshape(planes * size_y, size_z), basis_z, precision=TRANSFORM)
    return flat.reshape(planes, size_y, size_z)


def pair_average(size):
    rows = lax.broadcasted_iota(jnp.int32, (size, size // 2), 0)
    cols = lax.broadcasted_iota(jnp.int32, (size, size // 2), 1)
    return jnp.where(rows // 2 == cols, 0.5, 0.0).astype(jnp.float32)


def restrict(fields):
    count, planes, size_y, size_z = fields.shape
    pairs = fields.reshape(count, planes // 2, 2, size_y, size_z)
    summed = (pairs[:, :, 0] + pairs[:, :, 1]) * 0.5
    flat = jnp.dot(summed.reshape(-1, size_z), pair_average(size_z), precision=TRANSFORM)
    field = flat.reshape(count, planes // 2, size_y, size_z // 2)
    return jnp.einsum("ya,kpyz->kpaz", pair_average(size_y), field, precision=TRANSFORM)


def fetch(value, offset, back):
    count = lax.axis_size("space")
    if back == 0:
        pairs = [((target + offset) % count, target) for target in range(count)]
        return lax.ppermute(value, "space", pairs)
    slices = lax.axis_size("tm")
    pairs = [
        (((slot - back) % slices) * count + (target + offset) % count, slot * count + target)
        for slot in range(slices)
        for target in range(count)
    ]
    return lax.ppermute(value, ("tm", "space"), pairs)


def cover(low, high, have, local, allowed):
    plan = []
    at = low
    while at < high:
        best = None
        for offset in allowed:
            first = offset * local - have[0]
            last = offset * local + local + have[1]
            if first <= at < last and (best is None or last > best[2]):
                best = (offset, first, last)
        if best is None:
            offset = (at + have[0]) // local
            best = (offset, offset * local - have[0], offset * local + local + have[1])
        upto = min(best[2], high)
        plan.append((best[0], at - best[1], upto - best[1]))
        at = upto
    return plan


def gather_bands(items, back=0):
    local = items[0][0].shape[0] - items[0][1][0] - items[0][1][1]
    allowed = [0] if back == 0 else []
    plans = []
    for band, have, want in items:
        plan = cover(-want[0], local + want[1], have, local, allowed)
        for offset, _, _ in plan:
            if offset not in allowed:
                allowed.append(offset)
        plans.append(plan)
    by_offset = {}
    for i, plan in enumerate(plans):
        for j, (offset, first, last) in enumerate(plan):
            by_offset.setdefault(offset, []).append((i, j, first, last))
    got = {}
    for offset, entries in by_offset.items():
        parts = [items[i][0][first:last] for i, j, first, last in entries]
        if offset == 0 and back == 0:
            for (i, j, first, last), part in zip(entries, parts):
                got[(i, j)] = part
            continue
        moved = fetch(jnp.concatenate(parts, axis=0), offset, back)
        at = 0
        for i, j, first, last in entries:
            got[(i, j)] = moved[at:at + last - first]
            at += last - first
    return [
        jnp.concatenate([got[(i, j)] for j in range(len(plan))], axis=0)
        for i, plan in enumerate(plans)
    ]


def coarse_rate(ext):
    mid = ext[1:-1]
    lap = ext[2:] + ext[:-2]
    lap = lap + jnp.roll(mid, -1, 1) + jnp.roll(mid, 1, 1)
    lap = lap + jnp.roll(mid, -1, 2) + jnp.roll(mid, 1, 2)
    return EPS2 * ((lap - 6.0 * mid) * 0.25) + react(mid)


def spread(values, following, axis):
    middle = 0.5 * (values + following)
    both = jnp.stack([values, middle], axis=axis + 1)
    shape = list(values.shape)
    shape[axis] = shape[axis] * 2
    return both.reshape(shape)


def refine(stacked):
    matrix_y = interp_matrix(stacked.shape[2])
    matrix_z = interp_matrix(stacked.shape[3])
    both = jnp.einsum("kayc,zc->kayz", stacked, matrix_z, precision=TRANSFORM)
    both = jnp.einsum("Yy,kayz->kaYz", matrix_y, both, precision=TRANSFORM)
    planes = stacked.shape[1] - 1
    return spread(both[:, :planes], both[:, 1:], 1)


def coarse_sweep(start, rates, sums):
    first = start[1:-1] + 0.25 * (coarse_rate(start) - rates[0]) + sums[0]
    second = first[1:-1] + 0.25 * (coarse_rate(first) - rates[1]) + sums[1]
    return (first[1:-1], second)


def on_device(fine_nodes, fine_implicit):
    nodes = fine_nodes[0]
    implicit = fine_implicit[0]
    planes, size_y, size_z = (nodes.shape[1], nodes.shape[2], nodes.shape[3])
    devices = lax.axis_size("space")
    size_x = planes * devices
    local_y = size_y // devices
    basis_x = real_basis(size_x)
    basis_y = real_basis(size_y)
    basis_z = real_basis(size_z)
    columns = lax.axis_index("space") * local_y + lax.iota(jnp.int32, local_y)
    lam = wave_square(lax.iota(jnp.int32, size_x), size_x)[:, None, None]
    lam = lam + wave_square(columns, size_y)[None, :, None]
    lam = lam + wave_square(lax.iota(jnp.int32, size_z), size_z)[None, None, :]
    factor = 1.0 / (1.0 + 0.5 * lam)
    explicit_old = react(nodes)
    rates_old = explicit_old + implicit
    values = [nodes[0]]
    terms = [implicit[0]]
    for m in range(2):
        w = WEIGHTS[m]
        quad = 0.5 * (w[0] * rates_old[0] + w[1] * rates_old[1] + w[2] * rates_old[2])
        rhs = (
            values[m] + 0.25 * (react(values[m]) - explicit_old[m]) - 0.25 * implicit[m + 1] + quad
        )
        solved = spectral_solve(rhs, basis_x, basis_y, basis_z, factor)
        values.append(solved)
        terms.append((solved - rhs) * 4.0)
    fresh = jnp.stack(values)
    rates_new = react(fresh) + jnp.stack(terms)
    sums = [0.5 * (w[0] * rates_new[0] + w[1] * rates_new[1] + w[2] * rates_new[2]) for w in WEIGHTS]
    coarse = restrict(jnp.stack([values[0], values[1], values[2], sums[0], sums[1]]))
    slot = lax.axis_index("tm")
    slices = lax.axis_size("tm")
    local = planes // 2
    wide = gather_bands(
        [(coarse[0], (0, 0), (2, 3)), (coarse[1], (0, 0), (1, 2)), (coarse[3], (0, 0), (1, 2)),
         (coarse[4], (0, 0), (0, 1)), (coarse[2], (0, 0), (0, 1))]
    )
    start_c = wide[0]
    rates_c = (coarse_rate(start_c), coarse_rate(wide[1]))
    sums_c = (wide[2], wide[3])
    coarse_one = wide[1][1:2 + local]
    coarse_two = wide[4]
    start = start_c
    previous_coarse_two = None
    for section in range(slices - 1):
        first, second = coarse_sweep(start, rates_c, sums_c)
        items = [(second, (0, 1), (2, 3))]
        if previous_coarse_two is None:
            items.append((coarse_two, (0, 1), (0, 1)))
        received = gather_bands(items, back=1)
        if previous_coarse_two is None:
            previous_coarse_two = received[1]
        if section == slices - 2:
            previous_two, second = lax.optimization_barrier((values[2], second))
            previous_two = fetch(previous_two, 0, 1)
        start = jnp.where(slot == 0, start_c, received[0])
    first, second = coarse_sweep(start, rates_c, sums_c)
    delta = jnp.stack(
        [first - coarse_one, second - coarse_two,
         start[2:3 + local] - previous_coarse_two]
    )
    corr = refine(delta)
    fixed_one = values[1] + corr[0]
    fixed_two = values[2] + corr[1]
    head = jnp.where(slot == 0, nodes[0], previous_two + corr[2])
    return (jnp.stack([head, fixed_one, fixed_two])[None], jnp.stack([terms[1], terms[2]])[None])


def solution(mesh):
    return jax.shard_map(
        on_device,
        mesh=mesh,
        in_specs=(P("tm", None, "space", None, None), P("tm", None, "space", None, None)),
        out_specs=(P("tm", None, "space", None, None), P("tm", None, "space", None, None)),
        check_vma=False,
    )
```
